512 devices in a mesh: brick: 128 (over z, y, core), span: 4 (over x).
Axes of the slice: x: 4, y: 8, z: 8, core: 2. Of those that a mesh axis runs over, the one named last changes fastest.
Arguments:
- state: float32 [5, 128, 64, 1024], P(None, 'brick', 'span'), may hold values from -6 to 6
- jacobian_i: float32 [5, 5], replicated, may hold values from -2.5 to 2.5
- jacobian_j: float32 [5, 5], replicated, may hold values from -2.5 to 2.5
- brick_cols: int32 [128], P('brick'), may hold values from 1 to 1024, 81920 in all
- fringe_peer: int32 [128, 4, 2048], P('brick', 'span'), may hold values from 0 to 127, as said below
- fringe_donor: int32 [128, 4, 2048], P('brick', 'span'), may hold values from 0 to 15358, as said below
- fringe_target: int32 [128, 4, 2048], P('brick', 'span'), may hold values from 0 to 16383
- fringe_frac: float32 [2, 128, 4, 2048], P(None, 'brick', 'span'), may hold values from 0 to 1
- wall_patch: int32 [128, 4, 1024], P('brick', 'span'), may hold values from 0 to 16
- wall_angle: float32 [128, 4, 1024], P('brick', 'span'), may hold values from -3.140625 to 3.140625
Outputs:
- state_next: float32 [5, 128, 64, 1024], P(None, 'brick', 'span')
- loads: float32 [3, 16], replicated
The draws below stay inside these ranges and needn't reach their ends.
Inputs may be any that keep to these rules, and one draw needn't show every extreme that they name: `fringe_peer`: each device sends at most 32 rows to one brick index and exactly 32 to some; receptor targets are distinct on every receiving device. `fringe_donor`: i < 15 and j < 1023 for each donor corner.
All inputs are finite; a program needn't handle non-finite values. No bound on the sum of `brick_cols` on one device may be relied on, other than what follows from the above.
Results may differ from the reference program's by a relative error of at most 0.000071.
Values sent between devices are 32-bit elements; how exact they have to be, the bound alone decides.
No kernel may reach another device: no remote copies, remote signals or barrier semaphores. Data moves between devices by JAX's collectives and lax.ppermute only.
A program may use at most 128 MiB of HBM per device.

```python
import math
import jax
import jax.numpy as jnp
import numpy as np
from jax import lax

NVAR = 5
CI = 16
CJ = 1024
FR = 2048
NP = 16
NB = 128
NS = 4
NI = 64
CAP = 32
N_BRICK = 128


def fringe_plan(key):
    plan_key = jax.random.fold_in(key, 7)
    key_jitter, key_favored, key_shuffle, key_row, key_col = jax.random.split(plan_key, 5)
    slot_count = NB * CAP
    jitter = jax.random.randint(key_jitter, (NB, NS, slot_count), 0, 4096)
    peer_of = jnp.arange(slot_count, dtype=jnp.int32) // CAP
    source = jnp.arange(NB, dtype=jnp.int32)[:, None, None]
    distance = jnp.minimum((peer_of[None, None, :] - source) % NB, (source - peer_of[None, None, :]) % NB)
    nearness = jnp.maximum(0, 8 - distance) * 256
    favored = jax.random.randint(key_favored, (NB, NS, 1), 0, NB)
    scores = jnp.where(peer_of[None, None, :] == favored, 8191, jitter + nearness)
    ranked = scores * slot_count + jnp.arange(slot_count, dtype=jnp.int32)
    chosen = jnp.argsort(-ranked, axis=-1)[..., :FR].astype(jnp.int32)
    dest_peer = chosen // CAP
    within = chosen % CAP
    shuffles = jax.vmap(lambda k: jax.random.permutation(k, CI * CJ))(jax.random.split(key_shuffle, NB * NS))
    shuffles = shuffles.reshape(NB, NS, CI * CJ).astype(jnp.int32)
    slot_index = jnp.arange(NB, dtype=jnp.int32)[:, None, None] * CAP + within
    span_index = jnp.broadcast_to(jnp.arange(NS, dtype=jnp.int32)[None, :, None], dest_peer.shape)
    target = shuffles[dest_peer, span_index, slot_index]
    row_pick = jax.random.randint(key_row, (NB, NS, FR), 0, CI - 1)
    col_pick = jax.random.randint(key_col, (NB, NS, FR), 0, CJ - 1)
    donor_cell = row_pick * CJ + col_pick
    return (dest_peer.astype(jnp.int32), donor_cell.astype(jnp.int32), target.astype(jnp.int32))


def draw_fringe_peer(key, part):
    return fringe_plan(key)[0]


def draw_fringe_donor(key, part):
    return fringe_plan(key)[1]


def draw_fringe_target(key, part):
    return fringe_plan(key)[2]


def place_ends(result, key, least, top_value):
    extent = result.shape
    index_at = [jax.random.randint(jax.random.fold_in(key, axis), (), 0, extent[axis]) for axis in range(len(extent))]
    result = result.at[tuple(index_at)].set(least)
    longest = extent.index(max(extent))
    index_at[longest] = (index_at[longest] + 1) % extent[longest]
    return result.at[tuple(index_at)].set(top_value)


def shard_levels(key, dims, shards, least, top_value):
    level, own = 1.0, jax.random.fold_in(key, 6)
    for dim, parts in shards:
        heights = jnp.exp(jax.random.uniform(jax.random.fold_in(own, dim), (parts,), jnp.float32, least / len(shards), top_value / len(shards)))
        level = level * jnp.repeat(heights, dims[dim] // parts).reshape([-1 if axis == dim else 1 for axis in range(len(dims))])
    return level


def profile(number_of, total, bound, lean):
    weights = [(1 << 20) // math.isqrt(standing ** lean) + 1 for standing in range(2, number_of + 1)]
    surplus, given = total - bound - (number_of - 1), [1] * (number_of - 1)
    while surplus > 0:
        free = [i for i in range(number_of - 1) if given[i] < bound]
        pool, left = sum([weights[i] for i in free]), surplus
        for i in free:
            more = min(bound - given[i], max(1, left * weights[i] // pool), surplus)
            given[i] = given[i] + more
            surplus = surplus - more
    return np.array([bound] + given)


def ragged_sizes(key, number_of, total, most, lean):
    if number_of == 2:
        one = jax.random.randint(key, (), max(1, total - most), min(most, total - 1) + 1)
        return jnp.stack([one, total - one])
    tallies = jnp.asarray(profile(number_of, total, most, lean), jnp.int32)
    twos = (number_of - 1) // 2
    giver, receiver = tallies[1:1 + 2 * twos:2], tallies[2:2 + 2 * twos:2]
    room = jnp.minimum(giver - 1, most - receiver)
    passed = jax.random.randint(jax.random.fold_in(key, 1), (twos,), 0, 1 << 20) % (room + 1)
    tallies = tallies.at[1:1 + 2 * twos:2].set(giver - passed).at[2:2 + 2 * twos:2].set(receiver + passed)
    return tallies[jax.random.permutation(jax.random.fold_in(key, 2), number_of)]


def gaussian(stream_key, extent, spread, limit, cuts=(), kind=jnp.bfloat16):
    drawn = spread * jax.random.normal(stream_key, extent, jnp.float32)
    if cuts:
        drawn = drawn * shard_levels(stream_key, extent, cuts, -0.22, 0.18)
    return jnp.clip(drawn, -limit, limit).astype(kind)


def setup_inputs(seed: int = 0) -> dict:
    seeds = jax.random.split(jax.random.key(seed), 11)
    return {
        "state": gaussian(seeds[0], (NVAR, NB, NI, CJ), 1.0, 6.0, ((1, 128), (2, 4)), jnp.float32),
        "jacobian_i": gaussian(seeds[1], (NVAR, NVAR), NVAR ** -0.5, 2.5, (), jnp.float32),
        "jacobian_j": gaussian(seeds[2], (NVAR, NVAR), NVAR ** -0.5, 2.5, (), jnp.float32),
        "brick_cols": ragged_sizes(seeds[3], NB, N_BRICK * CJ * 5 // 8, CJ, 2).astype(jnp.int32),
        "fringe_peer": draw_fringe_peer(jax.random.fold_in(seeds[10], 71), 0),
        "fringe_donor": draw_fringe_donor(jax.random.fold_in(seeds[10], 71), 0),
        "fringe_target": draw_fringe_target(jax.random.fold_in(seeds[10], 71), 0),
        "fringe_frac": jnp.clip(1.0 * jax.random.uniform(seeds[7], (2, NB, NS, FR), jnp.float32) ** shard_levels(seeds[7], (2, NB, NS, FR), ((1, 128), (2, 4)), -0.2, 0.2), 0.0, 1.0),
        "wall_patch": place_ends(jax.random.randint(seeds[8], (NB, NS, CJ), 0, NP + 1), jax.random.fold_in(seeds[8], 1), 0, NP).astype(jnp.int32),
        "wall_angle": jnp.clip(jax.random.uniform(seeds[9], (NB, NS, CJ), jnp.float32, -3.140625, 3.140625), -3.140625, 3.140625),
    }


viscosity = 0.1
time_step = 0.3


def fringe_update(state, fringe_peer, fringe_donor, fringe_target, fringe_frac):
    flat_state = state.reshape(NVAR, NB, NS, CI * CJ)
    frac_a = fringe_frac[0][None]
    frac_c = fringe_frac[1][None]

    def corner(offset):
        return jnp.take_along_axis(flat_state, (fringe_donor + offset)[None].astype(jnp.int32), axis=3)

    interp = (1.0 - frac_a) * (1.0 - frac_c) * corner(0) + frac_a * (1.0 - frac_c) * corner(CJ)
    interp = interp + (1.0 - frac_a) * frac_c * corner(1) + frac_a * frac_c * corner(CJ + 1)
    span_index = jnp.broadcast_to(jnp.arange(NS, dtype=jnp.int32)[None, :, None], fringe_peer.shape)
    flat_state = flat_state.at[:, fringe_peer, span_index, fringe_target].set(interp)
    return flat_state.reshape(state.shape)


def residual_of(state, jacobian_i, jacobian_j, live_mask):
    padded = jnp.pad(state, ((0, 0), (0, 0), (1, 1), (1, 1)))
    diff_i = padded[:, :, 2:, 1:-1] - padded[:, :, :-2, 1:-1]
    diff_j = padded[:, :, 1:-1, 2:] - padded[:, :, 1:-1, :-2]
    laplace = padded[:, :, 2:, 1:-1] + padded[:, :, :-2, 1:-1] + padded[:, :, 1:-1, 2:] + padded[:, :, 1:-1, :-2] - 4.0 * state
    advect = jnp.einsum('vw,wbij->vbij', jacobian_i, diff_i, precision=lax.Precision.HIGHEST)
    advect = advect + jnp.einsum('vw,wbij->vbij', jacobian_j, diff_j, precision=lax.Precision.HIGHEST)
    return (-0.5 * advect + viscosity * laplace) * live_mask


def reference(state, jacobian_i, jacobian_j, brick_cols, fringe_peer, fringe_donor, fringe_target, fringe_frac, wall_patch, wall_angle):
    live_mask = (jnp.arange(CJ, dtype=jnp.int32)[None, :] < brick_cols[:, None]).astype(jnp.float32)[None, :, None, :]

    def fringe(field):
        return fringe_update(field, fringe_peer, fringe_donor, fringe_target, fringe_frac)

    def rhs(field):
        return residual_of(field, jacobian_i, jacobian_j, live_mask)

    section_zero = fringe(state)
    section_one = fringe(section_zero + time_step * rhs(section_zero))
    section_two = fringe(0.75 * section_zero + 0.25 * (section_one + time_step * rhs(section_one)))
    state_next = section_zero / 3.0 + (2.0 / 3.0) * (section_two + time_step * rhs(section_two))
    pressure = state_next[4][:, ::CI, :]
    xpos = (jnp.arange(CJ, dtype=jnp.float32) + 0.5) / CJ - 0.5
    force_x = pressure * jnp.cos(wall_angle)
    force_y = pressure * jnp.sin(wall_angle)
    moment = xpos * force_y
    onehot = (wall_patch[..., None] == jnp.arange(NP, dtype=jnp.int32)).astype(jnp.float32)
    contrib = jnp.stack([force_x, force_y, moment])
    loads = jnp.einsum('cbsj,bsjp->cp', contrib, onehot, precision=lax.Precision.HIGHEST) / CJ
    return state_next, loads
```

```python
import jax
import jax.numpy as jnp
from jax import lax
from jax.sharding import PartitionSpec as P

NP = 16

viscosity = 0.1
time_step = 0.3

F32 = jnp.float32
BF16 = jnp.bfloat16


def with_halo(block, axis, dim, width):
    count = lax.axis_size(axis)
    forward = [(i, i + 1) for i in range(count - 1)]
    backward = [(target, source) for source, target in forward]
    low = lax.ppermute(
        lax.slice_in_dim(block, block.shape[dim] - width, None, axis=dim), axis, forward
    )
    high = lax.ppermute(lax.slice_in_dim(block, 0, width, axis=dim), axis, backward)
    return jnp.concatenate([low, block, high], axis=dim)


def shift_cols(field, forward):
    zero_col = jnp.zeros(field.shape[:-1] + (1,), field.dtype)
    if forward:
        return jnp.concatenate([field[..., 1:], zero_col], axis=-1)
    return jnp.concatenate([zero_col, field[..., :-1]], axis=-1)


def split3(x):
    hi = lax.reduce_precision(x, exponent_bits=8, mantissa_bits=7)
    rest = x - hi
    mid = lax.reduce_precision(rest, exponent_bits=8, mantissa_bits=7)
    lo = rest - mid
    return jnp.stack([hi, mid, lo]).astype(BF16)


def join3(parts):
    return parts[0] + (parts[1] + parts[2])


def shards(
    state,
    jacobian_i,
    jacobian_j,
    brick_cols,
    fringe_peer,
    fringe_donor,
    fringe_target,
    fringe_frac,
    wall_patch,
    wall_angle,
):
    var_count = state.shape[0]
    row_count = state.shape[2]
    col_count = state.shape[3]
    peer_count = lax.axis_size("brick")
    fringe_rows = fringe_peer.shape[-1]
    capacity = 2 * fringe_rows // peer_count

    dest_peer = fringe_peer.reshape(fringe_rows)
    donor_cell = fringe_donor.reshape(fringe_rows)
    target_cell = fringe_target.reshape(fringe_rows)
    frac_a = fringe_frac[0].reshape(fringe_rows)
    frac_c = fringe_frac[1].reshape(fringe_rows)

    peer_hot = dest_peer[:, None] == jnp.arange(peer_count, dtype=jnp.int32)[None, :]
    peer_int = peer_hot.astype(jnp.int32)
    rank_in = jnp.sum(jnp.cumsum(peer_int, axis=0) * peer_int, axis=1) - 1
    peer_mat = peer_hot.astype(BF16)
    rank_hot = jnp.arange(capacity, dtype=jnp.int32)[:, None] == rank_in[None, :]

    donor_i = donor_cell // col_count
    donor_j = donor_cell % col_count
    col_mat = (jnp.arange(col_count, dtype=jnp.int32)[:, None] == donor_j[None, :]).astype(BF16)
    row_iota = jnp.arange(row_count, dtype=jnp.int32)[:, None]
    row_lo = row_iota == donor_i[None, :]
    row_hi = row_iota == donor_i[None, :] + 1

    def interpolate(field):
        shifted = jnp.concatenate([field[..., 1:], field[..., :1]], axis=-1)
        pieces = split3(jnp.stack([field, shifted]))
        picked = lax.dot_general(
            pieces, col_mat, (((4,), (0,)), ((), ())), preferred_element_type=F32
        )
        picked = join3(picked)
        at_lo = jnp.sum(jnp.where(row_lo[None, None], picked, 0.0), axis=2)
        at_hi = jnp.sum(jnp.where(row_hi[None, None], picked, 0.0), axis=2)
        q00, q01 = at_lo[0], at_lo[1]
        q10, q11 = at_hi[0], at_hi[1]
        a = frac_a[None]
        c = frac_c[None]
        interp = (1.0 - a) * (1.0 - c) * q00 + a * (1.0 - c) * q10
        return interp + (1.0 - a) * c * q01 + a * c * q11

    def exchange(values):
        pieces = split3(values)
        spread = jnp.where(rank_hot[None, None], pieces[:, :, None, :], jnp.zeros((), BF16))
        packed = lax.dot_general(
            peer_mat, spread, (((0,), (3,)), ((), ())), preferred_element_type=F32
        )
        packed = packed[:, 0] + (packed[:, 1] + packed[:, 2])
        return lax.all_to_all(packed, "brick", 0, 0, tiled=True)

    local_state = state[:, 0]

    first_interp = interpolate(local_state)
    target_code = (target_cell + 1).astype(F32)
    received = exchange(jnp.concatenate([first_interp, target_code[None]], axis=0))
    recv_cells = received[:, var_count].astype(jnp.int32) - 1
    recv_i = jnp.floor_divide(recv_cells, col_count)
    recv_j = recv_cells - recv_i * col_count
    cell_mat = (
        recv_j[:, :, None] == jnp.arange(col_count, dtype=jnp.int32)[None, None, :]
    ).astype(BF16)
    recv_row = jnp.arange(row_count, dtype=jnp.int32)[:, None, None] == recv_i[None]
    hit = lax.dot_general(
        recv_row.astype(BF16), cell_mat, (((1, 2), (0, 1)), ((), ())), preferred_element_type=F32
    )
    hit = hit > 0.5

    def place(field, values):
        pieces = split3(jnp.transpose(values, (1, 0, 2)))
        spread = jnp.where(recv_row[None, None], pieces[:, :, None], jnp.zeros((), BF16))
        placed = lax.dot_general(
            spread, cell_mat, (((3, 4), (0, 1)), ((), ())), preferred_element_type=F32
        )
        placed = join3(placed)
        return jnp.where(hit[None], placed, field)

    def fringe(field):
        return place(field, exchange(interpolate(field)))

    live_mask = (jnp.arange(col_count, dtype=jnp.int32) < brick_cols[0]).astype(F32)[None, None, :]

    def rhs(field):
        extended = with_halo(field, "span", 1, 1)
        upper = extended[:, 2:, :]
        lower = extended[:, :-2, :]
        right = shift_cols(field, True)
        left = shift_cols(field, False)
        diff_i = upper - lower
        diff_j = right - left
        laplace = upper + lower + right + left - 4.0 * field
        advect = jnp.einsum("vw,wij->vij", jacobian_i, diff_i, precision=lax.Precision.HIGHEST)
        advect = advect + jnp.einsum(
            "vw,wij->vij", jacobian_j, diff_j, precision=lax.Precision.HIGHEST
        )
        return (-0.5 * advect + viscosity * laplace) * live_mask

    section_zero = place(local_state, received[:, :var_count])
    section_one = fringe(section_zero + time_step * rhs(section_zero))
    section_two = fringe(0.75 * section_zero + 0.25 * (section_one + time_step * rhs(section_one)))
    state_next = section_zero / 3.0 + 2.0 / 3.0 * (section_two + time_step * rhs(section_two))
    pressure = state_next[4, 0, :]
    wall_dir = wall_angle.reshape(col_count)
    xpos = (jnp.arange(col_count, dtype=F32) + 0.5) / col_count - 0.5
    force_x = pressure * jnp.cos(wall_dir)
    force_y = pressure * jnp.sin(wall_dir)
    contrib = jnp.stack([force_x, force_y, xpos * force_y])
    patch_hot = (
        wall_patch.reshape(col_count)[:, None] == jnp.arange(NP, dtype=jnp.int32)[None, :]
    ).astype(F32)
    partial_loads = jnp.dot(contrib, patch_hot, precision=lax.Precision.HIGHEST)
    loads = lax.psum(partial_loads, ("brick", "span")) / col_count
    return (state_next[:, None], loads)


def solution(mesh):
    return jax.shard_map(
        shards,
        mesh=mesh,
        in_specs=(
            P(None, "brick", "span", None),
            P(),
            P(),
            P("brick"),
            P("brick", "span", None),
            P("brick", "span", None),
            P("brick", "span", None),
            P(None, "brick", "span", None),
            P("brick", "span", None),
            P("brick", "span", None),
        ),
        out_specs=(P(None, "brick", "span", None), P()),
        check_vma=False,
    )
```

```python
import jax
import jax.numpy as jnp
from jax import lax
from jax.sharding import PartitionSpec as P

NP = 16

viscosity = 0.1
time_step = 0.3

F32 = jnp.float32
BF16 = jnp.bfloat16


def with_halo(block, axis, dim, width):
    count = lax.axis_size(axis)
    forward = [(i, i + 1) for i in range(count - 1)]
    backward = [(target, source) for source, target in forward]
    low = lax.ppermute(
        lax.slice_in_dim(block, block.shape[dim] - width, None, axis=dim), axis, forward
    )
    high = lax.ppermute(lax.slice_in_dim(block, 0, width, axis=dim), axis, backward)
    return jnp.concatenate([low, block, high], axis=dim)


def shift_cols(field, forward):
    zero_col = jnp.zeros(field.shape[:-1] + (1,), field.dtype)
    if forward:
        return jnp.concatenate([field[..., 1:], zero_col], axis=-1)
    return jnp.concatenate([zero_col, field[..., :-1]], axis=-1)


def split3(x):
    hi = lax.reduce_precision(x, exponent_bits=8, mantissa_bits=7)
    rest = x - hi
    mid = lax.reduce_precision(rest, exponent_bits=8, mantissa_bits=7)
    lo = rest - mid
    return jnp.stack([hi, mid, lo]).astype(BF16)


def join3(parts):
    return parts[0] + (parts[1] + parts[2])


def shards(
    state,
    jacobian_i,
    jacobian_j,
    brick_cols,
    fringe_peer,
    fringe_donor,
    fringe_target,
    fringe_frac,
    wall_patch,
    wall_angle,
):
    var_count = state.shape[0]
    row_count = state.shape[2]
    col_count = state.shape[3]
    peer_count = lax.axis_size("brick")
    fringe_rows = fringe_peer.shape[-1]
    capacity = 2 * fringe_rows // peer_count

    dest_peer = fringe_peer.reshape(fringe_rows)
    donor_cell = fringe_donor.reshape(fringe_rows)
    target_cell = fringe_target.reshape(fringe_rows)
    frac_a = fringe_frac[0].reshape(fringe_rows)
    frac_c = fringe_frac[1].reshape(fringe_rows)

    peer_hot = dest_peer[:, None] == jnp.arange(peer_count, dtype=jnp.int32)[None, :]
    peer_int = peer_hot.astype(jnp.int32)
    rank_in = jnp.sum(jnp.cumsum(peer_int, axis=0) * peer_int, axis=1) - 1
    peer_mat = peer_hot.astype(BF16)
    rank_hot = jnp.arange(capacity, dtype=jnp.int32)[:, None] == rank_in[None, :]

    donor_i = donor_cell // col_count
    donor_j = donor_cell % col_count
    col_mat = (jnp.arange(col_count, dtype=jnp.int32)[:, None] == donor_j[None, :]).astype(BF16)
    row_iota = jnp.arange(row_count, dtype=jnp.int32)[:, None]
    row_lo = row_iota == donor_i[None, :]
    row_hi = row_iota == donor_i[None, :] + 1

    def interpolate(field):
        shifted = jnp.concatenate([field[..., 1:], field[..., :1]], axis=-1)
        pieces = split3(jnp.stack([field, shifted]))
        picked = lax.dot_general(
            pieces, col_mat, (((4,), (0,)), ((), ())), preferred_element_type=F32
        )
        picked = join3(picked)
        at_lo = jnp.sum(jnp.where(row_lo[None, None], picked, 0.0), axis=2)
        at_hi = jnp.sum(jnp.where(row_hi[None, None], picked, 0.0), axis=2)
        q00, q01 = at_lo[0], at_lo[1]
        q10, q11 = at_hi[0], at_hi[1]
        a = frac_a[None]
        c = frac_c[None]
        interp = (1.0 - a) * (1.0 - c) * q00 + a * (1.0 - c) * q10
        return interp + (1.0 - a) * c * q01 + a * c * q11

    def exchange(values):
        pieces = split3(values)
        spread = jnp.where(rank_hot[None, None], pieces[:, :, None, :], jnp.zeros((), BF16))
        packed = lax.dot_general(
            peer_mat, spread, (((0,), (3,)), ((), ())), preferred_element_type=F32
        )
        packed = packed[:, 0] + (packed[:, 1] + packed[:, 2])
        return lax.all_to_all(packed, "brick", 0, 0, tiled=True)

    local_state = state[:, 0]

    first_interp = interpolate(local_state)
    target_code = (target_cell + 1).astype(F32)
    received = exchange(jnp.concatenate([first_interp, target_code[None]], axis=0))
    recv_cells = received[:, var_count].astype(jnp.int32) - 1
    recv_i = jnp.floor_divide(recv_cells, col_count)
    recv_j = recv_cells - recv_i * col_count
    cell_mat = (
        recv_j[:, :, None] == jnp.arange(col_count, dtype=jnp.int32)[None, None, :]
    ).astype(BF16)
    recv_row = jnp.arange(row_count, dtype=jnp.int32)[:, None, None] == recv_i[None]
    hit = lax.dot_general(
        recv_row.astype(BF16), cell_mat, (((1, 2), (0, 1)), ((), ())), preferred_element_type=F32
    )
    hit = hit > 0.5

    def place(field, values):
        pieces = split3(jnp.transpose(values, (1, 0, 2)))
        spread = jnp.where(recv_row[None, None], pieces[:, :, None], jnp.zeros((), BF16))
        placed = lax.dot_general(
            spread, cell_mat, (((3, 4), (0, 1)), ((), ())), preferred_element_type=F32
        )
        placed = join3(placed)
        return jnp.where(hit[None], placed, field)

    def fringe(field):
        return place(field, exchange(interpolate(field)))

    live_mask = (jnp.arange(col_count, dtype=jnp.int32) < brick_cols[0]).astype(F32)[None, None, :]

    def rhs(field):
        extended = with_halo(field, "span", 1, 1)
        upper = extended[:, 2:, :]
        lower = extended[:, :-2, :]
        right = shift_cols(field, True)
        left = shift_cols(field, False)
        diff_i = upper - lower
        diff_j = right - left
        laplace = upper + lower + right + left - 4.0 * field
        advect = jnp.einsum("vw,wij->vij", jacobian_i, diff_i, precision=lax.Precision.HIGHEST)
        advect = advect + jnp.einsum(
            "vw,wij->vij", jacobian_j, diff_j, precision=lax.Precision.HIGHEST
        )
        return (-0.5 * advect + viscosity * laplace) * live_mask

    section_zero = place(local_state, received[:, :var_count])
    section_one = fringe(section_zero + time_step * rhs(section_zero))
    section_two = fringe(0.75 * section_zero + 0.25 * (section_one + time_step * rhs(section_one)))
    state_next = section_zero / 3.0 + 2.0 / 3.0 * (section_two + time_step * rhs(section_two))
    pressure = state_next[4, 0, :]
    wall_dir = wall_angle.reshape(col_count)
    xpos = (jnp.arange(col_count, dtype=F32) + 0.5) / col_count - 0.5
    force_x = pressure * jnp.cos(wall_dir)
    force_y = pressure * jnp.sin(wall_dir)
    contrib = jnp.stack([force_x, force_y, xpos * force_y])
    patch_hot = (
        wall_patch.reshape(col_count)[:, None] == jnp.arange(NP, dtype=jnp.int32)[None, :]
    ).astype(F32)
    partial_loads = jnp.dot(contrib, patch_hot, precision=lax.Precision.HIGHEST)
    device_count = lax.axis_size(("brick", "span"))
    copies = jnp.broadcast_to(partial_loads[None], (device_count,) + partial_loads.shape)
    gathered = lax.all_to_all(copies, ("brick", "span"), 0, 0, tiled=True)
    loads = jnp.sum(gathered, axis=0) / col_count
    return (state_next[:, None], loads)


def solution(mesh):
    return jax.shard_map(
        shards,
        mesh=mesh,
        in_specs=(
            P(None, "brick", "span", None),
            P(),
            P(),
            P("brick"),
            P("brick", "span", None),
            P("brick", "span", None),
            P("brick", "span", None),
            P(None, "brick", "span", None),
            P("brick", "span", None),
            P("brick", "span", None),
        ),
        out_specs=(P(None, "brick", "span", None), P()),
        check_vma=False,
    )
```

```python
import jax
import jax.numpy as jnp
from jax import lax
from jax.sharding import PartitionSpec as P

NP = 16

viscosity = 0.1
time_step = 0.3

F32 = jnp.float32
BF16 = jnp.bfloat16


def with_halo(block, axis, dim, width):
    count = lax.axis_size(axis)
    forward = [(i, i + 1) for i in range(count - 1)]
    backward = [(target, source) for source, target in forward]
    low = lax.ppermute(
        lax.slice_in_dim(block, block.shape[dim] - width, None, axis=dim), axis, forward
    )
    high = lax.ppermute(lax.slice_in_dim(block, 0, width, axis=dim), axis, backward)
    return jnp.concatenate([low, block, high], axis=dim)


def shift_cols(field, forward):
    zero_col = jnp.zeros(field.shape[:-1] + (1,), field.dtype)
    if forward:
        return jnp.concatenate([field[..., 1:], zero_col], axis=-1)
    return jnp.concatenate([zero_col, field[..., :-1]], axis=-1)


def split3(x):
    hi = lax.reduce_precision(x, exponent_bits=8, mantissa_bits=7)
    rest = x - hi
    mid = lax.reduce_precision(rest, exponent_bits=8, mantissa_bits=7)
    lo = rest - mid
    return jnp.stack([hi, mid, lo]).astype(BF16)


def join3(parts):
    return parts[0] + (parts[1] + parts[2])


def shards(
    state,
    jacobian_i,
    jacobian_j,
    brick_cols,
    fringe_peer,
    fringe_donor,
    fringe_target,
    fringe_frac,
    wall_patch,
    wall_angle,
):
    var_count = state.shape[0]
    row_count = state.shape[2]
    col_count = state.shape[3]
    peer_count = lax.axis_size("brick")
    fringe_rows = fringe_peer.shape[-1]
    capacity = 2 * fringe_rows // peer_count

    dest_peer = fringe_peer.reshape(fringe_rows)
    donor_cell = fringe_donor.reshape(fringe_rows)
    target_cell = fringe_target.reshape(fringe_rows)
    frac_a = fringe_frac[0].reshape(fringe_rows)
    frac_c = fringe_frac[1].reshape(fringe_rows)

    peer_hot = dest_peer[:, None] == jnp.arange(peer_count, dtype=jnp.int32)[None, :]
    peer_int = peer_hot.astype(jnp.int32)
    rank_in = jnp.sum(jnp.cumsum(peer_int, axis=0) * peer_int, axis=1) - 1
    peer_mat = peer_hot.astype(BF16)
    rank_hot = jnp.arange(capacity, dtype=jnp.int32)[:, None] == rank_in[None, :]

    donor_i = donor_cell // col_count
    donor_j = donor_cell % col_count
    col_mat = (jnp.arange(col_count, dtype=jnp.int32)[:, None] == donor_j[None, :]).astype(BF16)
    row_iota = jnp.arange(row_count, dtype=jnp.int32)[:, None]
    row_lo = row_iota == donor_i[None, :]
    row_hi = row_iota == donor_i[None, :] + 1

    def interpolate(field):
        shifted = jnp.concatenate([field[..., 1:], field[..., :1]], axis=-1)
        pieces = split3(jnp.stack([field, shifted]))
        picked = lax.dot_general(
            pieces, col_mat, (((4,), (0,)), ((), ())), preferred_element_type=F32
        )
        picked = join3(picked)
        at_lo = jnp.sum(jnp.where(row_lo[None, None], picked, 0.0), axis=2)
        at_hi = jnp.sum(jnp.where(row_hi[None, None], picked, 0.0), axis=2)
        q00, q01 = at_lo[0], at_lo[1]
        q10, q11 = at_hi[0], at_hi[1]
        a = frac_a[None]
        c = frac_c[None]
        interp = (1.0 - a) * (1.0 - c) * q00 + a * (1.0 - c) * q10
        return interp + (1.0 - a) * c * q01 + a * c * q11

    def exchange(values):
        pieces = split3(values)
        spread = jnp.where(rank_hot[None, None], pieces[:, :, None, :], jnp.zeros((), BF16))
        packed = lax.dot_general(
            peer_mat, spread, (((0,), (3,)), ((), ())), preferred_element_type=F32
        )
        packed = packed[:, 0] + (packed[:, 1] + packed[:, 2])
        return lax.all_to_all(packed, "brick", 0, 0, tiled=True)

    local_state = state[:, 0]

    first_interp = interpolate(local_state)
    target_code = (target_cell + 1).astype(F32)
    received = exchange(jnp.concatenate([first_interp, target_code[None]], axis=0))
    recv_cells = received[:, var_count].astype(jnp.int32) - 1
    recv_i = jnp.floor_divide(recv_cells, col_count)
    recv_j = recv_cells - recv_i * col_count
    cell_mat = (
        recv_j[:, :, None] == jnp.arange(col_count, dtype=jnp.int32)[None, None, :]
    ).astype(BF16)
    recv_row = jnp.arange(row_count, dtype=jnp.int32)[:, None, None] == recv_i[None]

    def spread_values(values):
        pieces = split3(jnp.transpose(values, (1, 0, 2)))
        return jnp.where(recv_row[None, None], pieces[:, :, None], jnp.zeros((), BF16))

    def to_cells(spread):
        return lax.dot_general(
            spread, cell_mat, (((3, 4), (0, 1)), ((), ())), preferred_element_type=F32
        )

    first_spread = spread_values(received[:, :var_count])
    marks = jnp.broadcast_to(recv_row.astype(BF16)[None, None], (3, 1) + recv_row.shape)
    first_cells = to_cells(jnp.concatenate([first_spread, marks], axis=1))
    hit = first_cells[0, var_count] > 0.5

    def place(field, values, cells=None):
        if cells is None:
            cells = to_cells(spread_values(values))
        placed = join3(cells)
        return jnp.where(hit[None], placed, field)

    def fringe(field):
        return place(field, exchange(interpolate(field)))

    live_mask = (jnp.arange(col_count, dtype=jnp.int32) < brick_cols[0]).astype(F32)[None, None, :]

    def rhs(field):
        extended = with_halo(field, "span", 1, 1)
        upper = extended[:, 2:, :]
        lower = extended[:, :-2, :]
        right = shift_cols(field, True)
        left = shift_cols(field, False)
        diff_i = upper - lower
        diff_j = right - left
        laplace = upper + lower + right + left - 4.0 * field
        advect = jnp.einsum("vw,wij->vij", jacobian_i, diff_i, precision=lax.Precision.HIGHEST)
        advect = advect + jnp.einsum(
            "vw,wij->vij", jacobian_j, diff_j, precision=lax.Precision.HIGHEST
        )
        return (-0.5 * advect + viscosity * laplace) * live_mask

    section_zero = place(local_state, None, first_cells[:, :var_count])
    section_one = fringe(section_zero + time_step * rhs(section_zero))
    section_two = fringe(0.75 * section_zero + 0.25 * (section_one + time_step * rhs(section_one)))
    state_next = section_zero / 3.0 + 2.0 / 3.0 * (section_two + time_step * rhs(section_two))
    pressure = state_next[4, 0, :]
    wall_dir = wall_angle.reshape(col_count)
    xpos = (jnp.arange(col_count, dtype=F32) + 0.5) / col_count - 0.5
    force_x = pressure * jnp.cos(wall_dir)
    force_y = pressure * jnp.sin(wall_dir)
    contrib = jnp.stack([force_x, force_y, xpos * force_y])
    patch_hot = (
        wall_patch.reshape(col_count)[:, None] == jnp.arange(NP, dtype=jnp.int32)[None, :]
    ).astype(F32)
    partial_loads = jnp.dot(contrib, patch_hot, precision=lax.Precision.HIGHEST)
    span_loads = lax.psum(partial_loads, "span")
    copies = jnp.broadcast_to(span_loads[None], (peer_count,) + span_loads.shape)
    gathered = lax.all_to_all(copies, "brick", 0, 0, tiled=True)
    loads = jnp.sum(gathered, axis=0) / col_count
    return (state_next[:, None], loads)


def solution(mesh):
    return jax.shard_map(
        shards,
        mesh=mesh,
        in_specs=(
            P(None, "brick", "span", None),
            P(),
            P(),
            P("brick"),
            P("brick", "span", None),
            P("brick", "span", None),
            P("brick", "span", None),
            P(None, "brick", "span", None),
            P("brick", "span", None),
            P("brick", "span", None),
        ),
        out_specs=(P(None, "brick", "span", None), P()),
        check_vma=False,
    )
```

```python
import jax
import jax.numpy as jnp
from jax import lax
from jax.sharding import PartitionSpec as P

NP = 16

viscosity = 0.1
time_step = 0.3

F32 = jnp.float32
BF16 = jnp.bfloat16


def with_halo(block, axis, dim, width):
    count = lax.axis_size(axis)
    forward = [(i, i + 1) for i in range(count - 1)]
    backward = [(target, source) for source, target in forward]
    low = lax.ppermute(
        lax.slice_in_dim(block, block.shape[dim] - width, None, axis=dim), axis, forward
    )
    high = lax.ppermute(lax.slice_in_dim(block, 0, width, axis=dim), axis, backward)
    return jnp.concatenate([low, block, high], axis=dim)


def shift_cols(field, forward):
    zero_col = jnp.zeros(field.shape[:-1] + (1,), field.dtype)
    if forward:
        return jnp.concatenate([field[..., 1:], zero_col], axis=-1)
    return jnp.concatenate([zero_col, field[..., :-1]], axis=-1)


def split_parts(x):
    hi = lax.reduce_precision(x, exponent_bits=8, mantissa_bits=7)
    lo = x - hi
    return jnp.stack([hi, lo]).astype(BF16)


def join_parts(parts):
    return parts[0] + parts[1]


def shards(
    state,
    jacobian_i,
    jacobian_j,
    brick_cols,
    fringe_peer,
    fringe_donor,
    fringe_target,
    fringe_frac,
    wall_patch,
    wall_angle,
):
    var_count = state.shape[0]
    row_count = state.shape[2]
    col_count = state.shape[3]
    peer_count = lax.axis_size("brick")
    fringe_rows = fringe_peer.shape[-1]
    capacity = 2 * fringe_rows // peer_count

    dest_peer = fringe_peer.reshape(fringe_rows)
    donor_cell = fringe_donor.reshape(fringe_rows)
    target_cell = fringe_target.reshape(fringe_rows)
    frac_a = fringe_frac[0].reshape(fringe_rows)
    frac_c = fringe_frac[1].reshape(fringe_rows)

    peer_hot = dest_peer[:, None] == jnp.arange(peer_count, dtype=jnp.int32)[None, :]
    peer_int = peer_hot.astype(jnp.int32)
    rank_in = jnp.sum(jnp.cumsum(peer_int, axis=0) * peer_int, axis=1) - 1
    peer_mat = peer_hot.astype(BF16)
    rank_hot = jnp.arange(capacity, dtype=jnp.int32)[:, None] == rank_in[None, :]

    donor_i = donor_cell // col_count
    donor_j = donor_cell % col_count
    col_mat = (jnp.arange(col_count, dtype=jnp.int32)[:, None] == donor_j[None, :]).astype(BF16)
    row_iota = jnp.arange(row_count, dtype=jnp.int32)[:, None]
    row_lo = row_iota == donor_i[None, :]
    row_hi = row_iota == donor_i[None, :] + 1

    def interpolate(field):
        shifted = jnp.concatenate([field[..., 1:], field[..., :1]], axis=-1)
        pieces = split_parts(jnp.stack([field, shifted]))
        picked = lax.dot_general(
            pieces, col_mat, (((4,), (0,)), ((), ())), preferred_element_type=F32
        )
        picked = join_parts(picked)
        at_lo = jnp.sum(jnp.where(row_lo[None, None], picked, 0.0), axis=2)
        at_hi = jnp.sum(jnp.where(row_hi[None, None], picked, 0.0), axis=2)
        q00, q01 = at_lo[0], at_lo[1]
        q10, q11 = at_hi[0], at_hi[1]
        a = frac_a[None]
        c = frac_c[None]
        interp = (1.0 - a) * (1.0 - c) * q00 + a * (1.0 - c) * q10
        return interp + (1.0 - a) * c * q01 + a * c * q11

    def exchange(values):
        pieces = split_parts(values)
        spread = jnp.where(rank_hot[None, None], pieces[:, :, None, :], jnp.zeros((), BF16))
        packed = lax.dot_general(
            peer_mat, spread, (((0,), (3,)), ((), ())), preferred_element_type=F32
        )
        packed = packed[:, 0] + packed[:, 1]
        return lax.all_to_all(packed, "brick", 0, 0, tiled=True)

    local_state = state[:, 0]

    first_interp = interpolate(local_state)
    target_code = (target_cell + 1).astype(F32)
    received = exchange(jnp.concatenate([first_interp, target_code[None]], axis=0))
    recv_cells = received[:, var_count].astype(jnp.int32) - 1
    recv_i = jnp.floor_divide(recv_cells, col_count)
    recv_j = recv_cells - recv_i * col_count
    cell_mat = (
        recv_j[:, :, None] == jnp.arange(col_count, dtype=jnp.int32)[None, None, :]
    ).astype(BF16)
    recv_row = jnp.arange(row_count, dtype=jnp.int32)[:, None, None] == recv_i[None]

    def spread_values(values):
        pieces = split_parts(jnp.transpose(values, (1, 0, 2)))
        return jnp.where(recv_row[None, None], pieces[:, :, None], jnp.zeros((), BF16))

    def to_cells(spread):
        return lax.dot_general(
            spread, cell_mat, (((3, 4), (0, 1)), ((), ())), preferred_element_type=F32
        )

    first_spread = spread_values(received[:, :var_count])
    marks = jnp.broadcast_to(recv_row.astype(BF16)[None, None], (2, 1) + recv_row.shape)
    first_cells = to_cells(jnp.concatenate([first_spread, marks], axis=1))
    hit = first_cells[0, var_count] > 0.5

    def place(field, values, cells=None):
        if cells is None:
            cells = to_cells(spread_values(values))
        placed = join_parts(cells)
        return jnp.where(hit[None], placed, field)

    def fringe(field):
        return place(field, exchange(interpolate(field)))

    live_mask = (jnp.arange(col_count, dtype=jnp.int32) < brick_cols[0]).astype(F32)[None, None, :]

    def rhs(field):
        extended = with_halo(field, "span", 1, 1)
        upper = extended[:, 2:, :]
        lower = extended[:, :-2, :]
        right = shift_cols(field, True)
        left = shift_cols(field, False)
        diff_i = upper - lower
        diff_j = right - left
        laplace = upper + lower + right + left - 4.0 * field
        advect = jnp.einsum("vw,wij->vij", jacobian_i, diff_i, precision=lax.Precision.HIGHEST)
        advect = advect + jnp.einsum(
            "vw,wij->vij", jacobian_j, diff_j, precision=lax.Precision.HIGHEST
        )
        return (-0.5 * advect + viscosity * laplace) * live_mask

    section_zero = place(local_state, None, first_cells[:, :var_count])
    section_one = fringe(section_zero + time_step * rhs(section_zero))
    section_two = fringe(0.75 * section_zero + 0.25 * (section_one + time_step * rhs(section_one)))
    state_next = section_zero / 3.0 + 2.0 / 3.0 * (section_two + time_step * rhs(section_two))
    pressure = state_next[4, 0, :]
    wall_dir = wall_angle.reshape(col_count)
    xpos = (jnp.arange(col_count, dtype=F32) + 0.5) / col_count - 0.5
    force_x = pressure * jnp.cos(wall_dir)
    force_y = pressure * jnp.sin(wall_dir)
    contrib = jnp.stack([force_x, force_y, xpos * force_y])
    patch_hot = (
        wall_patch.reshape(col_count)[:, None] == jnp.arange(NP, dtype=jnp.int32)[None, :]
    ).astype(F32)
    partial_loads = jnp.dot(contrib, patch_hot, precision=lax.Precision.HIGHEST)
    span_loads = lax.psum(partial_loads, "span")
    copies = jnp.broadcast_to(span_loads[None], (peer_count,) + span_loads.shape)
    gathered = lax.all_to_all(copies, "brick", 0, 0, tiled=True)
    loads = jnp.sum(gathered, axis=0) / col_count
    return (state_next[:, None], loads)


def solution(mesh):
    return jax.shard_map(
        shards,
        mesh=mesh,
        in_specs=(
            P(None, "brick", "span", None),
            P(),
            P(),
            P("brick"),
            P("brick", "span", None),
            P("brick", "span", None),
            P("brick", "span", None),
            P(None, "brick", "span", None),
            P("brick", "span", None),
            P("brick", "span", None),
        ),
        out_specs=(P(None, "brick", "span", None), P()),
        check_vma=False,
    )
```

```python
import jax
import jax.numpy as jnp
from jax import lax
from jax.sharding import PartitionSpec as P

NP = 16

viscosity = 0.1
time_step = 0.3

F32 = jnp.float32
BF16 = jnp.bfloat16


def with_halo(block, axis, dim, width):
    count = lax.axis_size(axis)
    forward = [(i, i + 1) for i in range(count - 1)]
    backward = [(target, source) for source, target in forward]
    low = lax.ppermute(
        lax.slice_in_dim(block, block.shape[dim] - width, None, axis=dim), axis, forward
    )
    high = lax.ppermute(lax.slice_in_dim(block, 0, width, axis=dim), axis, backward)
    return jnp.concatenate([low, block, high], axis=dim)


def shift_cols(field, forward):
    zero_col = jnp.zeros(field.shape[:-1] + (1,), field.dtype)
    if forward:
        return jnp.concatenate([field[..., 1:], zero_col], axis=-1)
    return jnp.concatenate([zero_col, field[..., :-1]], axis=-1)


def split_parts(x):
    hi = lax.reduce_precision(x, exponent_bits=8, mantissa_bits=7)
    lo = x - hi
    return jnp.stack([hi, lo]).astype(BF16)


def join_parts(parts):
    return parts[0] + parts[1]


def shards(
    state,
    jacobian_i,
    jacobian_j,
    brick_cols,
    fringe_peer,
    fringe_donor,
    fringe_target,
    fringe_frac,
    wall_patch,
    wall_angle,
):
    var_count = state.shape[0]
    row_count = state.shape[2]
    col_count = state.shape[3]
    peer_count = lax.axis_size("brick")
    fringe_rows = fringe_peer.shape[-1]
    capacity = 2 * fringe_rows // peer_count

    dest_peer = fringe_peer.reshape(fringe_rows)
    donor_cell = fringe_donor.reshape(fringe_rows)
    target_cell = fringe_target.reshape(fringe_rows)
    frac_a = fringe_frac[0].reshape(fringe_rows)
    frac_c = fringe_frac[1].reshape(fringe_rows)

    peer_hot = dest_peer[:, None] == jnp.arange(peer_count, dtype=jnp.int32)[None, :]
    peer_int = peer_hot.astype(jnp.int32)
    rank_in = jnp.sum(jnp.cumsum(peer_int, axis=0) * peer_int, axis=1) - 1
    peer_mat = peer_hot.astype(BF16)
    rank_hot = jnp.arange(capacity, dtype=jnp.int32)[:, None] == rank_in[None, :]

    donor_i = donor_cell // col_count
    donor_j = donor_cell % col_count
    col_mat = (jnp.arange(col_count, dtype=jnp.int32)[:, None] == donor_j[None, :]).astype(BF16)
    row_iota = jnp.arange(row_count, dtype=jnp.int32)[:, None]
    row_lo = row_iota == donor_i[None, :]
    row_hi = row_iota == donor_i[None, :] + 1

    def interpolate(field):
        shifted = jnp.concatenate([field[..., 1:], field[..., :1]], axis=-1)
        pieces = split_parts(jnp.stack([field, shifted]))
        picked = lax.dot_general(
            pieces, col_mat, (((4,), (0,)), ((), ())), preferred_element_type=F32
        )
        picked = join_parts(picked)
        at_lo = jnp.sum(jnp.where(row_lo[None, None], picked, 0.0), axis=2)
        at_hi = jnp.sum(jnp.where(row_hi[None, None], picked, 0.0), axis=2)
        q00, q01 = at_lo[0], at_lo[1]
        q10, q11 = at_hi[0], at_hi[1]
        a = frac_a[None]
        c = frac_c[None]
        interp = (1.0 - a) * (1.0 - c) * q00 + a * (1.0 - c) * q10
        return interp + (1.0 - a) * c * q01 + a * c * q11

    def exchange(values):
        pieces = split_parts(values)
        spread = jnp.where(rank_hot[None, None], pieces[:, :, None, :], jnp.zeros((), BF16))
        packed = lax.dot_general(
            peer_mat, spread, (((0,), (3,)), ((), ())), preferred_element_type=F32
        )
        packed = packed[:, 0] + packed[:, 1]
        return lax.all_to_all(packed, "brick", 0, 0, tiled=True)

    local_state = state[:, 0]

    first_interp = interpolate(local_state)
    target_code = (target_cell + 1).astype(F32)
    received = exchange(jnp.concatenate([first_interp, target_code[None]], axis=0))
    recv_cells = received[:, var_count].astype(jnp.int32) - 1
    recv_i = jnp.floor_divide(recv_cells, col_count)
    recv_j = recv_cells - recv_i * col_count
    cell_mat = (
        recv_j[:, :, None] == jnp.arange(col_count, dtype=jnp.int32)[None, None, :]
    ).astype(BF16)
    recv_row = jnp.arange(row_count, dtype=jnp.int32)[:, None, None] == recv_i[None]

    def spread_values(values):
        pieces = split_parts(jnp.transpose(values, (1, 0, 2)))
        return jnp.where(recv_row[None, None], pieces[:, :, None], jnp.zeros((), BF16))

    def to_cells(spread):
        return lax.dot_general(
            spread, cell_mat, (((3, 4), (0, 1)), ((), ())), preferred_element_type=F32
        )

    first_spread = spread_values(received[:, :var_count])
    marks = jnp.broadcast_to(recv_row.astype(BF16)[None, None], (2, 1) + recv_row.shape)
    first_cells = to_cells(jnp.concatenate([first_spread, marks], axis=1))
    hit = first_cells[0, var_count] > 0.5

    def place(field, values, cells=None):
        if cells is None:
            cells = to_cells(spread_values(values))
        placed = join_parts(cells)
        return jnp.where(hit[None], placed, field)

    def fringe(field):
        return place(field, exchange(interpolate(field)))

    live_mask = (jnp.arange(col_count, dtype=jnp.int32) < brick_cols[0]).astype(F32)[None, None, :]

    def rhs(field):
        extended = with_halo(field, "span", 1, 1)
        upper = extended[:, 2:, :]
        lower = extended[:, :-2, :]
        right = shift_cols(field, True)
        left = shift_cols(field, False)
        diff_i = upper - lower
        diff_j = right - left
        laplace = upper + lower + right + left - 4.0 * field
        advect = jnp.einsum("vw,wij->vij", jacobian_i, diff_i, precision=lax.Precision.HIGHEST)
        advect = advect + jnp.einsum(
            "vw,wij->vij", jacobian_j, diff_j, precision=lax.Precision.HIGHEST
        )
        return (-0.5 * advect + viscosity * laplace) * live_mask

    section_zero = place(local_state, None, first_cells[:, :var_count])
    section_one = fringe(section_zero + time_step * rhs(section_zero))
    section_two = fringe(0.75 * section_zero + 0.25 * (section_one + time_step * rhs(section_one)))
    state_next = section_zero / 3.0 + 2.0 / 3.0 * (section_two + time_step * rhs(section_two))
    span_count = lax.axis_size("span")
    wall_dir = wall_angle.reshape(col_count)
    own_geom = jnp.stack(
        [(wall_patch.reshape(col_count) + 1).astype(F32), jnp.cos(wall_dir), jnp.sin(wall_dir)]
    )
    next_geom = lax.ppermute(own_geom, "span", [(i + 1, i) for i in range(span_count - 1)])
    xpos = (jnp.arange(col_count, dtype=F32) + 0.5) / col_count - 0.5
    live_row = live_mask[0, 0]

    def wall_partial(pressure, geom):
        patch = geom[0].astype(jnp.int32) - 1
        patch_hot = (patch[:, None] == jnp.arange(NP, dtype=jnp.int32)[None, :]).astype(F32)
        force_x = pressure * geom[1]
        force_y = pressure * geom[2]
        contrib = jnp.stack([force_x, force_y, xpos * force_y])
        return jnp.dot(contrib, patch_hot, precision=lax.Precision.HIGHEST)

    first = section_two[:, 0]
    diff_j = shift_cols(first, True) - shift_cols(first, False)
    laplace = section_two[4, 1] + shift_cols(first[4], True) + shift_cols(first[4], False)
    laplace = laplace - 4.0 * first[4]
    advect = jnp.dot(jacobian_i[4], section_two[:, 1], precision=lax.Precision.HIGHEST)
    advect = advect + jnp.dot(jacobian_j[4], diff_j, precision=lax.Precision.HIGHEST)
    own_rate = (-0.5 * advect + viscosity * laplace) * live_row
    own_pressure = section_zero[4, 0] / 3.0 + 2.0 / 3.0 * (first[4] + time_step * own_rate)
    last = section_two[:, -1]
    halo_rate = (0.5 * jnp.dot(jacobian_i[4], last, precision=lax.Precision.HIGHEST) + viscosity * last[4]) * live_row
    next_pressure = 2.0 / 3.0 * (time_step * halo_rate)
    partial_loads = wall_partial(own_pressure, own_geom) + wall_partial(next_pressure, next_geom)
    span_loads = lax.psum(partial_loads, "span")
    copies = jnp.broadcast_to(span_loads[None], (peer_count,) + span_loads.shape)
    gathered = lax.all_to_all(copies, "brick", 0, 0, tiled=True)
    loads = jnp.sum(gathered, axis=0) / col_count
    return (state_next[:, None], loads)


def solution(mesh):
    return jax.shard_map(
        shards,
        mesh=mesh,
        in_specs=(
            P(None, "brick", "span", None),
            P(),
            P(),
            P("brick"),
            P("brick", "span", None),
            P("brick", "span", None),
            P("brick", "span", None),
            P(None, "brick", "span", None),
            P("brick", "span", None),
            P("brick", "span", None),
        ),
        out_specs=(P(None, "brick", "span", None), P()),
        check_vma=False,
    )
```

```python
import jax
import jax.numpy as jnp
from jax import lax
from jax.sharding import PartitionSpec as P

NP = 16

viscosity = 0.1
time_step = 0.3

F32 = jnp.float32
BF16 = jnp.bfloat16


def with_halo(block, axis, dim, width):
    count = lax.axis_size(axis)
    forward = [(i, i + 1) for i in range(count - 1)]
    backward = [(target, source) for source, target in forward]
    low = lax.ppermute(
        lax.slice_in_dim(block, block.shape[dim] - width, None, axis=dim), axis, forward
    )
    high = lax.ppermute(lax.slice_in_dim(block, 0, width, axis=dim), axis, backward)
    return jnp.concatenate([low, block, high], axis=dim)


def shift_cols(field, forward):
    zero_col = jnp.zeros(field.shape[:-1] + (1,), field.dtype)
    if forward:
        return jnp.concatenate([field[..., 1:], zero_col], axis=-1)
    return jnp.concatenate([zero_col, field[..., :-1]], axis=-1)


def split_parts(x):
    hi = lax.reduce_precision(x, exponent_bits=8, mantissa_bits=7)
    lo = x - hi
    return jnp.stack([hi, lo]).astype(BF16)


def join_parts(parts):
    return parts[0] + parts[1]


def shards(
    state,
    jacobian_i,
    jacobian_j,
    brick_cols,
    fringe_peer,
    fringe_donor,
    fringe_target,
    fringe_frac,
    wall_patch,
    wall_angle,
):
    var_count = state.shape[0]
    row_count = state.shape[2]
    col_count = state.shape[3]
    peer_count = lax.axis_size("brick")
    fringe_rows = fringe_peer.shape[-1]
    capacity = 2 * fringe_rows // peer_count

    dest_peer = fringe_peer.reshape(fringe_rows)
    donor_cell = fringe_donor.reshape(fringe_rows)
    target_cell = fringe_target.reshape(fringe_rows)
    frac_a = fringe_frac[0].reshape(fringe_rows)
    frac_c = fringe_frac[1].reshape(fringe_rows)

    peer_hot = dest_peer[:, None] == jnp.arange(peer_count, dtype=jnp.int32)[None, :]
    peer_int = peer_hot.astype(jnp.int32)
    rank_in = jnp.sum(jnp.cumsum(peer_int, axis=0) * peer_int, axis=1) - 1
    peer_mat = peer_hot.astype(BF16)
    rank_hot = jnp.arange(capacity, dtype=jnp.int32)[:, None] == rank_in[None, :]

    donor_i = donor_cell // col_count
    donor_j = donor_cell % col_count
    col_mat = (jnp.arange(col_count, dtype=jnp.int32)[:, None] == donor_j[None, :]).astype(
        jnp.float8_e4m3fn
    )
    col_mat = lax.optimization_barrier(col_mat)
    row_iota = jnp.arange(row_count, dtype=jnp.int32)[:, None]
    row_lo = row_iota == donor_i[None, :]
    row_hi = row_iota == donor_i[None, :] + 1

    def interpolate(field):
        shifted = jnp.concatenate([field[..., 1:], field[..., :1]], axis=-1)
        pieces = split_parts(jnp.stack([field, shifted]))
        picked = lax.dot_general(
            pieces, col_mat.astype(BF16), (((4,), (0,)), ((), ())), preferred_element_type=F32
        )
        picked = join_parts(picked)
        at_lo = jnp.sum(jnp.where(row_lo[None, None], picked, 0.0), axis=2)
        at_hi = jnp.sum(jnp.where(row_hi[None, None], picked, 0.0), axis=2)
        q00, q01 = at_lo[0], at_lo[1]
        q10, q11 = at_hi[0], at_hi[1]
        a = frac_a[None]
        c = frac_c[None]
        interp = (1.0 - a) * (1.0 - c) * q00 + a * (1.0 - c) * q10
        return interp + (1.0 - a) * c * q01 + a * c * q11

    def exchange(values):
        pieces = split_parts(values)
        spread = jnp.where(rank_hot[None, None], pieces[:, :, None, :], jnp.zeros((), BF16))
        packed = lax.dot_general(
            peer_mat, spread, (((0,), (3,)), ((), ())), preferred_element_type=F32
        )
        packed = packed[:, 0] + packed[:, 1]
        return lax.all_to_all(packed, "brick", 0, 0, tiled=True)

    local_state = state[:, 0]

    first_interp = interpolate(local_state)
    target_code = (target_cell + 1).astype(F32)
    received = exchange(jnp.concatenate([first_interp, target_code[None]], axis=0))
    recv_cells = received[:, var_count].astype(jnp.int32) - 1
    recv_i = jnp.floor_divide(recv_cells, col_count)
    recv_j = recv_cells - recv_i * col_count
    cell_mat = (
        recv_j[:, :, None] == jnp.arange(col_count, dtype=jnp.int32)[None, None, :]
    ).astype(jnp.float8_e4m3fn)
    cell_mat = lax.optimization_barrier(cell_mat)
    recv_row = jnp.arange(row_count, dtype=jnp.int32)[:, None, None] == recv_i[None]

    def spread_values(values):
        pieces = split_parts(jnp.transpose(values, (1, 0, 2)))
        return jnp.where(recv_row[None, None], pieces[:, :, None], jnp.zeros((), BF16))

    def to_cells(spread):
        return lax.dot_general(
            spread, cell_mat.astype(BF16), (((3, 4), (0, 1)), ((), ())), preferred_element_type=F32
        )

    first_spread = spread_values(received[:, :var_count])
    marks = jnp.broadcast_to(recv_row.astype(BF16)[None, None], (2, 1) + recv_row.shape)
    first_cells = to_cells(jnp.concatenate([first_spread, marks], axis=1))
    hit = first_cells[0, var_count] > 0.5

    def place(field, values, cells=None):
        if cells is None:
            cells = to_cells(spread_values(values))
        placed = join_parts(cells)
        return jnp.where(hit[None], placed, field)

    def fringe(field):
        return place(field, exchange(interpolate(field)))

    live_mask = (jnp.arange(col_count, dtype=jnp.int32) < brick_cols[0]).astype(F32)[None, None, :]

    def rhs(field):
        extended = with_halo(field, "span", 1, 1)
        upper = extended[:, 2:, :]
        lower = extended[:, :-2, :]
        right = shift_cols(field, True)
        left = shift_cols(field, False)
        diff_i = upper - lower
        diff_j = right - left
        laplace = upper + lower + right + left - 4.0 * field
        advect = jnp.einsum("vw,wij->vij", jacobian_i, diff_i, precision=lax.Precision.HIGHEST)
        advect = advect + jnp.einsum(
            "vw,wij->vij", jacobian_j, diff_j, precision=lax.Precision.HIGHEST
        )
        return (-0.5 * advect + viscosity * laplace) * live_mask

    section_zero = place(local_state, None, first_cells[:, :var_count])
    section_one = fringe(section_zero + time_step * rhs(section_zero))
    section_two = fringe(0.75 * section_zero + 0.25 * (section_one + time_step * rhs(section_one)))
    state_next = section_zero / 3.0 + 2.0 / 3.0 * (section_two + time_step * rhs(section_two))
    span_count = lax.axis_size("span")
    wall_dir = wall_angle.reshape(col_count)
    own_geom = jnp.stack(
        [(wall_patch.reshape(col_count) + 1).astype(F32), jnp.cos(wall_dir), jnp.sin(wall_dir)]
    )
    next_geom = lax.ppermute(own_geom, "span", [(i + 1, i) for i in range(span_count - 1)])
    xpos = (jnp.arange(col_count, dtype=F32) + 0.5) / col_count - 0.5
    live_row = live_mask[0, 0]

    def wall_partial(pressure, geom):
        patch = geom[0].astype(jnp.int32) - 1
        patch_hot = (patch[:, None] == jnp.arange(NP, dtype=jnp.int32)[None, :]).astype(F32)
        force_x = pressure * geom[1]
        force_y = pressure * geom[2]
        contrib = jnp.stack([force_x, force_y, xpos * force_y])
        return jnp.dot(contrib, patch_hot, precision=lax.Precision.HIGHEST)

    first = section_two[:, 0]
    diff_j = shift_cols(first, True) - shift_cols(first, False)
    laplace = section_two[4, 1] + shift_cols(first[4], True) + shift_cols(first[4], False)
    laplace = laplace - 4.0 * first[4]
    advect = jnp.dot(jacobian_i[4], section_two[:, 1], precision=lax.Precision.HIGHEST)
    advect = advect + jnp.dot(jacobian_j[4], diff_j, precision=lax.Precision.HIGHEST)
    own_rate = (-0.5 * advect + viscosity * laplace) * live_row
    own_pressure = section_zero[4, 0] / 3.0 + 2.0 / 3.0 * (first[4] + time_step * own_rate)
    last = section_two[:, -1]
    halo_rate = (0.5 * jnp.dot(jacobian_i[4], last, precision=lax.Precision.HIGHEST) + viscosity * last[4]) * live_row
    next_pressure = 2.0 / 3.0 * (time_step * halo_rate)
    partial_loads = wall_partial(own_pressure, own_geom) + wall_partial(next_pressure, next_geom)
    span_loads = lax.psum(partial_loads, "span")
    copies = jnp.broadcast_to(span_loads[None], (peer_count,) + span_loads.shape)
    gathered = lax.all_to_all(copies, "brick", 0, 0, tiled=True)
    loads = jnp.sum(gathered, axis=0) / col_count
    return (state_next[:, None], loads)


def solution(mesh):
    return jax.shard_map(
        shards,
        mesh=mesh,
        in_specs=(
            P(None, "brick", "span", None),
            P(),
            P(),
            P("brick"),
            P("brick", "span", None),
            P("brick", "span", None),
            P("brick", "span", None),
            P(None, "brick", "span", None),
            P("brick", "span", None),
            P("brick", "span", None),
        ),
        out_specs=(P(None, "brick", "span", None), P()),
        check_vma=False,
    )
```

```python
import jax
import jax.numpy as jnp
from jax import lax
from jax.sharding import PartitionSpec as P

NP = 16

viscosity = 0.1
time_step = 0.3

F32 = jnp.float32
BF16 = jnp.bfloat16


def shift_cols(field, forward):
    zero_col = jnp.zeros(field.shape[:-1] + (1,), field.dtype)
    if forward:
        return jnp.concatenate([field[..., 1:], zero_col], axis=-1)
    return jnp.concatenate([zero_col, field[..., :-1]], axis=-1)


def split_parts(x):
    hi = lax.reduce_precision(x, exponent_bits=8, mantissa_bits=7)
    lo = x - hi
    return jnp.stack([hi, lo]).astype(BF16)


def join_parts(parts):
    return parts[0] + parts[1]


def shards(
    state,
    jacobian_i,
    jacobian_j,
    brick_cols,
    fringe_peer,
    fringe_donor,
    fringe_target,
    fringe_frac,
    wall_patch,
    wall_angle,
):
    var_count = state.shape[0]
    row_count = state.shape[2]
    col_count = state.shape[3]
    peer_count = lax.axis_size("brick")
    fringe_rows = fringe_peer.shape[-1]
    capacity = 2 * fringe_rows // peer_count

    dest_peer = fringe_peer.reshape(fringe_rows)
    donor_cell = fringe_donor.reshape(fringe_rows)
    target_cell = fringe_target.reshape(fringe_rows)
    frac_a = fringe_frac[0].reshape(fringe_rows)
    frac_c = fringe_frac[1].reshape(fringe_rows)

    peer_hot = dest_peer[:, None] == jnp.arange(peer_count, dtype=jnp.int32)[None, :]
    peer_int = peer_hot.astype(jnp.int32)
    rank_in = jnp.sum(jnp.cumsum(peer_int, axis=0) * peer_int, axis=1) - 1
    peer_mat = peer_hot.astype(BF16)
    rank_hot = jnp.arange(capacity, dtype=jnp.int32)[:, None] == rank_in[None, :]

    donor_i = donor_cell // col_count
    donor_j = donor_cell % col_count
    col_mat = (jnp.arange(col_count, dtype=jnp.int32)[:, None] == donor_j[None, :]).astype(BF16)
    row_iota = jnp.arange(row_count, dtype=jnp.int32)[:, None]
    row_lo = row_iota == donor_i[None, :]
    row_hi = row_iota == donor_i[None, :] + 1

    def interpolate(field):
        shifted = jnp.concatenate([field[..., 1:], field[..., :1]], axis=-1)
        pieces = split_parts(jnp.stack([field, shifted]))
        picked = lax.dot_general(
            pieces, col_mat, (((4,), (0,)), ((), ())), preferred_element_type=F32
        )
        picked = join_parts(picked)
        at_lo = jnp.sum(jnp.where(row_lo[None, None], picked, 0.0), axis=2)
        at_hi = jnp.sum(jnp.where(row_hi[None, None], picked, 0.0), axis=2)
        q00, q01 = at_lo[0], at_lo[1]
        q10, q11 = at_hi[0], at_hi[1]
        a = frac_a[None]
        c = frac_c[None]
        interp = (1.0 - a) * (1.0 - c) * q00 + a * (1.0 - c) * q10
        return interp + (1.0 - a) * c * q01 + a * c * q11

    def exchange(values):
        pieces = split_parts(values)
        spread = jnp.where(rank_hot[None, None], pieces[:, :, None, :], jnp.zeros((), BF16))
        packed = lax.dot_general(
            peer_mat, spread, (((0,), (3,)), ((), ())), preferred_element_type=F32
        )
        packed = packed[:, 0] + packed[:, 1]
        return lax.all_to_all(packed, "brick", 0, 0, tiled=True)

    local_state = state[:, 0]

    first_interp = interpolate(local_state)
    target_code = (target_cell + 1).astype(F32)
    received = exchange(jnp.concatenate([first_interp, target_code[None]], axis=0))
    recv_cells = received[:, var_count].astype(jnp.int32) - 1
    recv_i = jnp.floor_divide(recv_cells, col_count)
    recv_j = recv_cells - recv_i * col_count
    cell_mat = (
        recv_j[:, :, None] == jnp.arange(col_count, dtype=jnp.int32)[None, None, :]
    ).astype(BF16)
    recv_row = jnp.arange(row_count, dtype=jnp.int32)[:, None, None] == recv_i[None]

    def spread_values(values):
        pieces = split_parts(jnp.transpose(values, (1, 0, 2)))
        return jnp.where(recv_row[None, None], pieces[:, :, None], jnp.zeros((), BF16))

    def to_cells(spread):
        return lax.dot_general(
            spread, cell_mat, (((3, 4), (0, 1)), ((), ())), preferred_element_type=F32
        )

    first_spread = spread_values(received[:, :var_count])
    marks = jnp.broadcast_to(recv_row.astype(BF16)[None, None], (2, 1) + recv_row.shape)
    first_cells = to_cells(jnp.concatenate([first_spread, marks], axis=1))
    hit = first_cells[0, var_count] > 0.5

    def place(field, values, cells=None):
        if cells is None:
            cells = to_cells(spread_values(values))
        placed = join_parts(cells)
        return jnp.where(hit[None], placed, field)

    def fringe(field):
        return place(field, exchange(interpolate(field)))

    live_mask = (jnp.arange(col_count, dtype=jnp.int32) < brick_cols[0]).astype(F32)[None, None, :]

    def rhs(field, extra=None):
        count = lax.axis_size("span")
        forward = [(i, i + 1) for i in range(count - 1)]
        backward = [(target, source) for source, target in forward]
        low = lax.ppermute(field[:, -1:], "span", forward)
        sent = field[:, :1] if extra is None else jnp.concatenate([field[:, :1], extra[:, None]])
        high = lax.ppermute(sent, "span", backward)
        upper = jnp.concatenate([field[:, 1:], high[: field.shape[0]]], axis=1)
        lower = jnp.concatenate([low, field[:, :-1]], axis=1)
        right = shift_cols(field, True)
        left = shift_cols(field, False)
        diff_i = upper - lower
        diff_j = right - left
        laplace = upper + lower + right + left - 4.0 * field
        advect = jnp.einsum("vw,wij->vij", jacobian_i, diff_i, precision=lax.Precision.HIGHEST)
        advect = advect + jnp.einsum(
            "vw,wij->vij", jacobian_j, diff_j, precision=lax.Precision.HIGHEST
        )
        rate = (-0.5 * advect + viscosity * laplace) * live_mask
        return rate if extra is None else (rate, high[field.shape[0] :, 0])

    wall_dir = wall_angle.reshape(col_count)
    own_geom = jnp.stack(
        [(wall_patch.reshape(col_count) + 1).astype(F32), jnp.cos(wall_dir), jnp.sin(wall_dir)]
    )

    section_zero = place(local_state, None, first_cells[:, :var_count])
    zero_rate, next_geom = rhs(section_zero, own_geom)
    section_one = fringe(section_zero + time_step * zero_rate)
    section_two = fringe(0.75 * section_zero + 0.25 * (section_one + time_step * rhs(section_one)))
    state_next = section_zero / 3.0 + 2.0 / 3.0 * (section_two + time_step * rhs(section_two))
    xpos = (jnp.arange(col_count, dtype=F32) + 0.5) / col_count - 0.5
    live_row = live_mask[0, 0]

    def wall_partial(pressure, geom):
        patch = geom[0].astype(jnp.int32) - 1
        patch_hot = (patch[:, None] == jnp.arange(NP, dtype=jnp.int32)[None, :]).astype(F32)
        force_x = pressure * geom[1]
        force_y = pressure * geom[2]
        contrib = jnp.stack([force_x, force_y, xpos * force_y])
        return jnp.dot(contrib, patch_hot, precision=lax.Precision.HIGHEST)

    first = section_two[:, 0]
    diff_j = shift_cols(first, True) - shift_cols(first, False)
    laplace = section_two[4, 1] + shift_cols(first[4], True) + shift_cols(first[4], False)
    laplace = laplace - 4.0 * first[4]
    advect = jnp.dot(jacobian_i[4], section_two[:, 1], precision=lax.Precision.HIGHEST)
    advect = advect + jnp.dot(jacobian_j[4], diff_j, precision=lax.Precision.HIGHEST)
    own_rate = (-0.5 * advect + viscosity * laplace) * live_row
    own_pressure = section_zero[4, 0] / 3.0 + 2.0 / 3.0 * (first[4] + time_step * own_rate)
    last = section_two[:, -1]
    halo_rate = (0.5 * jnp.dot(jacobian_i[4], last, precision=lax.Precision.HIGHEST) + viscosity * last[4]) * live_row
    next_pressure = 2.0 / 3.0 * (time_step * halo_rate)
    partial_loads = wall_partial(own_pressure, own_geom) + wall_partial(next_pressure, next_geom)
    span_loads = lax.psum(partial_loads, "span")
    copies = jnp.broadcast_to(span_loads[None], (peer_count,) + span_loads.shape)
    gathered = lax.all_to_all(copies, "brick", 0, 0, tiled=True)
    loads = jnp.sum(gathered, axis=0) / col_count
    return (state_next[:, None], loads)


def solution(mesh):
    return jax.shard_map(
        shards,
        mesh=mesh,
        in_specs=(
            P(None, "brick", "span", None),
            P(),
            P(),
            P("brick"),
            P("brick", "span", None),
            P("brick", "span", None),
            P("brick", "span", None),
            P(None, "brick", "span", None),
            P("brick", "span", None),
            P("brick", "span", None),
        ),
        out_specs=(P(None, "brick", "span", None), P()),
        check_vma=False,
    )
```

```python
import jax
import jax.numpy as jnp
from jax import lax
from jax.sharding import PartitionSpec as P

NP = 16

viscosity = 0.1
time_step = 0.3

F32 = jnp.float32
BF16 = jnp.bfloat16


def with_halo(block, axis, dim, width):
    count = lax.axis_size(axis)
    forward = [(i, i + 1) for i in range(count - 1)]
    backward = [(target, source) for source, target in forward]
    low = lax.ppermute(
        lax.slice_in_dim(block, block.shape[dim] - width, None, axis=dim), axis, forward
    )
    high = lax.ppermute(lax.slice_in_dim(block, 0, width, axis=dim), axis, backward)
    return jnp.concatenate([low, block, high], axis=dim)


def shift_cols(field, forward):
    zero_col = jnp.zeros(field.shape[:-1] + (1,), field.dtype)
    if forward:
        return jnp.concatenate([field[..., 1:], zero_col], axis=-1)
    return jnp.concatenate([zero_col, field[..., :-1]], axis=-1)


def split_parts(x):
    hi = lax.reduce_precision(x, exponent_bits=8, mantissa_bits=7)
    lo = x - hi
    return jnp.stack([hi, lo]).astype(BF16)


def join_parts(parts):
    return parts[0] + parts[1]


def shards(
    state,
    jacobian_i,
    jacobian_j,
    brick_cols,
    fringe_peer,
    fringe_donor,
    fringe_target,
    fringe_frac,
    wall_patch,
    wall_angle,
):
    var_count = state.shape[0]
    row_count = state.shape[2]
    col_count = state.shape[3]
    peer_count = lax.axis_size("brick")
    fringe_rows = fringe_peer.shape[-1]
    capacity = 2 * fringe_rows // peer_count

    dest_peer = fringe_peer.reshape(fringe_rows)
    donor_cell = fringe_donor.reshape(fringe_rows)
    target_cell = fringe_target.reshape(fringe_rows)
    frac_a = fringe_frac[0].reshape(fringe_rows)
    frac_c = fringe_frac[1].reshape(fringe_rows)

    peer_hot = dest_peer[:, None] == jnp.arange(peer_count, dtype=jnp.int32)[None, :]
    peer_int = peer_hot.astype(jnp.int32)
    rank_in = jnp.sum(jnp.cumsum(peer_int, axis=0) * peer_int, axis=1) - 1
    peer_mat = peer_hot.astype(BF16)
    rank_hot = jnp.arange(capacity, dtype=jnp.int32)[:, None] == rank_in[None, :]

    donor_i = donor_cell // col_count
    donor_j = donor_cell % col_count
    col_mat = (jnp.arange(col_count, dtype=jnp.int32)[:, None] == donor_j[None, :]).astype(BF16)
    row_iota = jnp.arange(row_count, dtype=jnp.int32)[:, None]
    row_lo = row_iota == donor_i[None, :]
    row_hi = row_iota == donor_i[None, :] + 1

    def interpolate(field):
        shifted = jnp.concatenate([field[..., 1:], field[..., :1]], axis=-1)
        pieces = split_parts(jnp.stack([field, shifted]))
        picked = lax.dot_general(
            pieces, col_mat, (((4,), (0,)), ((), ())), preferred_element_type=F32
        )
        picked = join_parts(picked)
        at_lo = jnp.sum(jnp.where(row_lo[None, None], picked, 0.0), axis=2)
        at_hi = jnp.sum(jnp.where(row_hi[None, None], picked, 0.0), axis=2)
        q00, q01 = at_lo[0], at_lo[1]
        q10, q11 = at_hi[0], at_hi[1]
        a = frac_a[None]
        c = frac_c[None]
        interp = (1.0 - a) * (1.0 - c) * q00 + a * (1.0 - c) * q10
        return interp + (1.0 - a) * c * q01 + a * c * q11

    def exchange(values):
        pieces = split_parts(values)
        spread = jnp.where(rank_hot[None, None], pieces[:, :, None, :], jnp.zeros((), BF16))
        packed = lax.dot_general(
            peer_mat, spread, (((0,), (3,)), ((), ())), preferred_element_type=F32
        )
        packed = packed[:, 0] + packed[:, 1]
        return lax.all_to_all(packed, "brick", 0, 0, tiled=True)

    local_state = state[:, 0]

    first_interp = interpolate(local_state)
    target_code = (target_cell + 1).astype(F32)
    received = exchange(jnp.concatenate([first_interp, target_code[None]], axis=0))
    slot_count = peer_count * capacity

    def flat_slots(values):
        return jnp.transpose(values, (1, 0, 2)).reshape(values.shape[1], slot_count)

    recv_cells = flat_slots(received[:, var_count:]).astype(jnp.int32)[0] - 1
    recv_i = jnp.floor_divide(recv_cells, col_count)
    recv_j = recv_cells - recv_i * col_count
    cell_mat = (
        recv_j[:, None] == jnp.arange(col_count, dtype=jnp.int32)[None, :]
    ).astype(BF16)
    recv_row = jnp.arange(row_count, dtype=jnp.int32)[:, None] == recv_i[None]

    def spread_values(values):
        pieces = split_parts(flat_slots(values))
        return jnp.where(recv_row[None, None], pieces[:, :, None], jnp.zeros((), BF16))

    def to_cells(spread):
        return lax.dot_general(
            spread, cell_mat, (((3,), (0,)), ((), ())), preferred_element_type=F32
        )

    first_spread = spread_values(received[:, :var_count])
    marks = jnp.broadcast_to(recv_row.astype(BF16)[None, None], (2, 1) + recv_row.shape)
    first_cells = to_cells(jnp.concatenate([first_spread, marks], axis=1))
    hit = first_cells[0, var_count] > 0.5

    def place(field, values, cells=None):
        if cells is None:
            cells = to_cells(spread_values(values))
        placed = join_parts(cells)
        return jnp.where(hit[None], placed, field)

    def fringe(field):
        return place(field, exchange(interpolate(field)))

    live_mask = (jnp.arange(col_count, dtype=jnp.int32) < brick_cols[0]).astype(F32)[None, None, :]

    def rhs(field):
        extended = with_halo(field, "span", 1, 1)
        upper = extended[:, 2:, :]
        lower = extended[:, :-2, :]
        right = shift_cols(field, True)
        left = shift_cols(field, False)
        diff_i = upper - lower
        diff_j = right - left
        laplace = upper + lower + right + left - 4.0 * field
        advect = jnp.einsum("vw,wij->vij", jacobian_i, diff_i, precision=lax.Precision.HIGHEST)
        advect = advect + jnp.einsum(
            "vw,wij->vij", jacobian_j, diff_j, precision=lax.Precision.HIGHEST
        )
        return (-0.5 * advect + viscosity * laplace) * live_mask

    section_zero = place(local_state, None, first_cells[:, :var_count])
    section_one = fringe(section_zero + time_step * rhs(section_zero))
    section_two = fringe(0.75 * section_zero + 0.25 * (section_one + time_step * rhs(section_one)))
    state_next = section_zero / 3.0 + 2.0 / 3.0 * (section_two + time_step * rhs(section_two))
    span_count = lax.axis_size("span")
    wall_dir = wall_angle.reshape(col_count)
    own_geom = jnp.stack(
        [(wall_patch.reshape(col_count) + 1).astype(F32), jnp.cos(wall_dir), jnp.sin(wall_dir)]
    )
    next_geom = lax.ppermute(own_geom, "span", [(i + 1, i) for i in range(span_count - 1)])
    xpos = (jnp.arange(col_count, dtype=F32) + 0.5) / col_count - 0.5
    live_row = live_mask[0, 0]

    def wall_partial(pressure, geom):
        patch = geom[0].astype(jnp.int32) - 1
        patch_hot = (patch[:, None] == jnp.arange(NP, dtype=jnp.int32)[None, :]).astype(F32)
        force_x = pressure * geom[1]
        force_y = pressure * geom[2]
        contrib = jnp.stack([force_x, force_y, xpos * force_y])
        return jnp.dot(contrib, patch_hot, precision=lax.Precision.HIGHEST)

    first = section_two[:, 0]
    diff_j = shift_cols(first, True) - shift_cols(first, False)
    laplace = section_two[4, 1] + shift_cols(first[4], True) + shift_cols(first[4], False)
    laplace = laplace - 4.0 * first[4]
    advect = jnp.dot(jacobian_i[4], section_two[:, 1], precision=lax.Precision.HIGHEST)
    advect = advect + jnp.dot(jacobian_j[4], diff_j, precision=lax.Precision.HIGHEST)
    own_rate = (-0.5 * advect + viscosity * laplace) * live_row
    own_pressure = section_zero[4, 0] / 3.0 + 2.0 / 3.0 * (first[4] + time_step * own_rate)
    last = section_two[:, -1]
    halo_rate = (0.5 * jnp.dot(jacobian_i[4], last, precision=lax.Precision.HIGHEST) + viscosity * last[4]) * live_row
    next_pressure = 2.0 / 3.0 * (time_step * halo_rate)
    partial_loads = wall_partial(own_pressure, own_geom) + wall_partial(next_pressure, next_geom)
    span_loads = lax.psum(partial_loads, "span")
    copies = jnp.broadcast_to(span_loads[None], (peer_count,) + span_loads.shape)
    gathered = lax.all_to_all(copies, "brick", 0, 0, tiled=True)
    loads = jnp.sum(gathered, axis=0) / col_count
    return (state_next[:, None], loads)


def solution(mesh):
    return jax.shard_map(
        shards,
        mesh=mesh,
        in_specs=(
            P(None, "brick", "span", None),
            P(),
            P(),
            P("brick"),
            P("brick", "span", None),
            P("brick", "span", None),
            P("brick", "span", None),
            P(None, "brick", "span", None),
            P("brick", "span", None),
            P("brick", "span", None),
        ),
        out_specs=(P(None, "brick", "span", None), P()),
        check_vma=False,
    )
```

```python
import jax
import jax.numpy as jnp
from jax import lax
from jax.sharding import PartitionSpec as P

NP = 16

viscosity = 0.1
time_step = 0.3

F32 = jnp.float32
BF16 = jnp.bfloat16


def with_halo(block, axis, dim, width):
    count = lax.axis_size(axis)
    forward = [(i, i + 1) for i in range(count - 1)]
    backward = [(target, source) for source, target in forward]
    low = lax.ppermute(
        lax.slice_in_dim(block, block.shape[dim] - width, None, axis=dim), axis, forward
    )
    high = lax.ppermute(lax.slice_in_dim(block, 0, width, axis=dim), axis, backward)
    return jnp.concatenate([low, block, high], axis=dim)


def shift_cols(field, forward):
    zero_col = jnp.zeros(field.shape[:-1] + (1,), field.dtype)
    if forward:
        return jnp.concatenate([field[..., 1:], zero_col], axis=-1)
    return jnp.concatenate([zero_col, field[..., :-1]], axis=-1)


def split_parts(x):
    hi = lax.reduce_precision(x, exponent_bits=8, mantissa_bits=7)
    lo = x - hi
    return jnp.stack([hi, lo]).astype(BF16)


def join_parts(parts):
    return parts[0] + parts[1]


def shards(
    state,
    jacobian_i,
    jacobian_j,
    brick_cols,
    fringe_peer,
    fringe_donor,
    fringe_target,
    fringe_frac,
    wall_patch,
    wall_angle,
):
    var_count = state.shape[0]
    row_count = state.shape[2]
    col_count = state.shape[3]
    peer_count = lax.axis_size("brick")
    fringe_rows = fringe_peer.shape[-1]
    capacity = 2 * fringe_rows // peer_count

    dest_peer = fringe_peer.reshape(fringe_rows)
    donor_cell = fringe_donor.reshape(fringe_rows)
    target_cell = fringe_target.reshape(fringe_rows)
    frac_a = fringe_frac[0].reshape(fringe_rows)
    frac_c = fringe_frac[1].reshape(fringe_rows)

    peer_hot = dest_peer[:, None] == jnp.arange(peer_count, dtype=jnp.int32)[None, :]
    peer_int = peer_hot.astype(jnp.int32)
    rank_in = jnp.sum(jnp.cumsum(peer_int, axis=0) * peer_int, axis=1) - 1
    peer_mat = peer_hot.astype(BF16)
    rank_hot = jnp.arange(capacity, dtype=jnp.int32)[:, None] == rank_in[None, :]

    donor_i = donor_cell // col_count
    donor_j = donor_cell % col_count
    col_mat = (jnp.arange(col_count, dtype=jnp.int32)[:, None] == donor_j[None, :]).astype(BF16)
    row_iota = jnp.arange(row_count, dtype=jnp.int32)[:, None]
    row_lo = row_iota == donor_i[None, :]
    row_hi = row_iota == donor_i[None, :] + 1

    def interpolate(field):
        shifted = jnp.concatenate([field[..., 1:], field[..., :1]], axis=-1)
        pieces = split_parts(jnp.stack([field, shifted]))
        picked = lax.dot_general(
            pieces, col_mat, (((4,), (0,)), ((), ())), preferred_element_type=F32
        )
        picked = join_parts(picked)
        at_lo = jnp.sum(jnp.where(row_lo[None, None], picked, 0.0), axis=2)
        at_hi = jnp.sum(jnp.where(row_hi[None, None], picked, 0.0), axis=2)
        q00, q01 = at_lo[0], at_lo[1]
        q10, q11 = at_hi[0], at_hi[1]
        a = frac_a[None]
        c = frac_c[None]
        interp = (1.0 - a) * (1.0 - c) * q00 + a * (1.0 - c) * q10
        return interp + (1.0 - a) * c * q01 + a * c * q11

    def exchange(values):
        pieces = split_parts(values)
        spread = jnp.where(rank_hot[None, None], pieces[:, :, None, :], jnp.zeros((), BF16))
        packed = lax.dot_general(
            peer_mat, spread, (((0,), (3,)), ((), ())), preferred_element_type=F32
        )
        packed = packed[:, 0] + packed[:, 1]
        return lax.all_to_all(packed, "brick", 0, 0, tiled=True)

    local_state = state[:, 0]

    first_interp = interpolate(local_state)
    target_code = (target_cell + 1).astype(F32)
    received = exchange(jnp.concatenate([first_interp, target_code[None]], axis=0))
    slot_count = peer_count * capacity

    def flat_slots(values):
        return jnp.transpose(values, (1, 0, 2)).reshape(values.shape[1], slot_count)

    recv_cells = flat_slots(received[:, var_count:]).astype(jnp.int32)[0] - 1
    recv_i = jnp.floor_divide(recv_cells, col_count)
    recv_j = recv_cells - recv_i * col_count
    cell_mat = (
        recv_j[:, None] == jnp.arange(col_count, dtype=jnp.int32)[None, :]
    ).astype(BF16)
    recv_row = jnp.arange(row_count, dtype=jnp.int32)[:, None] == recv_i[None]

    def spread_values(values):
        pieces = split_parts(flat_slots(values))
        return jnp.where(recv_row[None, None], pieces[:, :, None], jnp.zeros((), BF16))

    def to_cells(spread):
        return lax.dot_general(
            spread, cell_mat, (((3,), (0,)), ((), ())), preferred_element_type=F32
        )

    first_spread = spread_values(received[:, :var_count])
    marks = jnp.broadcast_to(recv_row.astype(BF16)[None, None], (2, 1) + recv_row.shape)
    first_cells = to_cells(jnp.concatenate([first_spread, marks], axis=1))
    hit = first_cells[0, var_count] > 0.5

    def place(field, values, cells=None):
        if cells is None:
            cells = to_cells(spread_values(values))
        placed = join_parts(cells)
        return jnp.where(hit[None], placed, field)

    def fringe(field):
        return place(field, exchange(interpolate(field)))

    live_mask = (jnp.arange(col_count, dtype=jnp.int32) < brick_cols[0]).astype(F32)[None, None, :]

    def rhs(field):
        extended = with_halo(field, "span", 1, 1)
        upper = extended[:, 2:, :]
        lower = extended[:, :-2, :]
        right = shift_cols(field, True)
        left = shift_cols(field, False)
        diff_i = upper - lower
        diff_j = right - left
        laplace = upper + lower + right + left - 4.0 * field
        advect = jnp.einsum("vw,wij->vij", jacobian_i, diff_i, precision=lax.Precision.HIGHEST)
        advect = advect + jnp.einsum(
            "vw,wij->vij", jacobian_j, diff_j, precision=lax.Precision.HIGHEST
        )
        return (-0.5 * advect + viscosity * laplace) * live_mask

    section_zero = place(local_state, None, first_cells[:, :var_count])
    keep_of = jnp.array([0.0, 0.75], F32)
    blend_of = jnp.array([1.0, 0.25], F32)

    def section(step, field):
        stage = field + time_step * rhs(field)
        return fringe(keep_of[step] * section_zero + blend_of[step] * stage)

    section_two = lax.fori_loop(0, 2, section, section_zero)
    state_next = section_zero / 3.0 + 2.0 / 3.0 * (section_two + time_step * rhs(section_two))
    span_count = lax.axis_size("span")
    wall_dir = wall_angle.reshape(col_count)
    own_geom = jnp.stack(
        [(wall_patch.reshape(col_count) + 1).astype(F32), jnp.cos(wall_dir), jnp.sin(wall_dir)]
    )
    next_geom = lax.ppermute(own_geom, "span", [(i + 1, i) for i in range(span_count - 1)])
    xpos = (jnp.arange(col_count, dtype=F32) + 0.5) / col_count - 0.5
    live_row = live_mask[0, 0]

    def wall_partial(pressure, geom):
        patch = geom[0].astype(jnp.int32) - 1
        patch_hot = (patch[:, None] == jnp.arange(NP, dtype=jnp.int32)[None, :]).astype(F32)
        force_x = pressure * geom[1]
        force_y = pressure * geom[2]
        contrib = jnp.stack([force_x, force_y, xpos * force_y])
        return jnp.dot(contrib, patch_hot, precision=lax.Precision.HIGHEST)

    first = section_two[:, 0]
    diff_j = shift_cols(first, True) - shift_cols(first, False)
    laplace = section_two[4, 1] + shift_cols(first[4], True) + shift_cols(first[4], False)
    laplace = laplace - 4.0 * first[4]
    advect = jnp.dot(jacobian_i[4], section_two[:, 1], precision=lax.Precision.HIGHEST)
    advect = advect + jnp.dot(jacobian_j[4], diff_j, precision=lax.Precision.HIGHEST)
    own_rate = (-0.5 * advect + viscosity * laplace) * live_row
    own_pressure = section_zero[4, 0] / 3.0 + 2.0 / 3.0 * (first[4] + time_step * own_rate)
    last = section_two[:, -1]
    halo_rate = (0.5 * jnp.dot(jacobian_i[4], last, precision=lax.Precision.HIGHEST) + viscosity * last[4]) * live_row
    next_pressure = 2.0 / 3.0 * (time_step * halo_rate)
    partial_loads = wall_partial(own_pressure, own_geom) + wall_partial(next_pressure, next_geom)
    span_loads = lax.psum(partial_loads, "span")
    copies = jnp.broadcast_to(span_loads[None], (peer_count,) + span_loads.shape)
    gathered = lax.all_to_all(copies, "brick", 0, 0, tiled=True)
    loads = jnp.sum(gathered, axis=0) / col_count
    return (state_next[:, None], loads)


def solution(mesh):
    return jax.shard_map(
        shards,
        mesh=mesh,
        in_specs=(
            P(None, "brick", "span", None),
            P(),
            P(),
            P("brick"),
            P("brick", "span", None),
            P("brick", "span", None),
            P("brick", "span", None),
            P(None, "brick", "span", None),
            P("brick", "span", None),
            P("brick", "span", None),
        ),
        out_specs=(P(None, "brick", "span", None), P()),
        check_vma=False,
    )
```

```python
import jax
import jax.numpy as jnp
from jax import lax
from jax.sharding import PartitionSpec as P

NP = 16

viscosity = 0.1
time_step = 0.3

F32 = jnp.float32
BF16 = jnp.bfloat16


def with_halo(block, axis, dim, width):
    count = lax.axis_size(axis)
    forward = [(i, i + 1) for i in range(count - 1)]
    backward = [(target, source) for source, target in forward]
    low = lax.ppermute(
        lax.slice_in_dim(block, block.shape[dim] - width, None, axis=dim), axis, forward
    )
    high = lax.ppermute(lax.slice_in_dim(block, 0, width, axis=dim), axis, backward)
    return jnp.concatenate([low, block, high], axis=dim)


def shift_cols(field, forward):
    zero_col = jnp.zeros(field.shape[:-1] + (1,), field.dtype)
    if forward:
        return jnp.concatenate([field[..., 1:], zero_col], axis=-1)
    return jnp.concatenate([zero_col, field[..., :-1]], axis=-1)


def split_parts(x):
    hi = lax.reduce_precision(x, exponent_bits=8, mantissa_bits=7)
    lo = x - hi
    return jnp.stack([hi, lo]).astype(BF16)


def join_parts(parts):
    return parts[0] + parts[1]


def shards(
    state,
    jacobian_i,
    jacobian_j,
    brick_cols,
    fringe_peer,
    fringe_donor,
    fringe_target,
    fringe_frac,
    wall_patch,
    wall_angle,
):
    var_count = state.shape[0]
    row_count = state.shape[2]
    col_count = state.shape[3]
    peer_count = lax.axis_size("brick")
    fringe_rows = fringe_peer.shape[-1]
    capacity = 2 * fringe_rows // peer_count

    dest_peer = fringe_peer.reshape(fringe_rows)
    donor_cell = fringe_donor.reshape(fringe_rows)
    target_cell = fringe_target.reshape(fringe_rows)
    frac_a = fringe_frac[0].reshape(fringe_rows)
    frac_c = fringe_frac[1].reshape(fringe_rows)

    peer_hot = dest_peer[:, None] == jnp.arange(peer_count, dtype=jnp.int32)[None, :]
    peer_int = peer_hot.astype(jnp.int32)
    rank_in = jnp.sum(jnp.cumsum(peer_int, axis=0) * peer_int, axis=1) - 1
    peer_mat = peer_hot.astype(BF16)
    rank_hot = jnp.arange(capacity, dtype=jnp.int32)[:, None] == rank_in[None, :]

    donor_i = donor_cell // col_count
    donor_j = donor_cell % col_count
    col_mat = (jnp.arange(col_count, dtype=jnp.int32)[:, None] == donor_j[None, :]).astype(
        jnp.float8_e4m3fn
    )
    col_mat = lax.optimization_barrier(col_mat)
    row_iota = jnp.arange(row_count, dtype=jnp.int32)[:, None]
    row_lo = row_iota == donor_i[None, :]
    row_hi = row_iota == donor_i[None, :] + 1

    def interpolate(field):
        shifted = jnp.concatenate([field[..., 1:], field[..., :1]], axis=-1)
        pieces = split_parts(jnp.stack([field, shifted]))
        picked = lax.dot_general(
            pieces, col_mat.astype(BF16), (((4,), (0,)), ((), ())), preferred_element_type=F32
        )
        picked = join_parts(picked)
        at_lo = jnp.sum(jnp.where(row_lo[None, None], picked, 0.0), axis=2)
        at_hi = jnp.sum(jnp.where(row_hi[None, None], picked, 0.0), axis=2)
        q00, q01 = at_lo[0], at_lo[1]
        q10, q11 = at_hi[0], at_hi[1]
        a = frac_a[None]
        c = frac_c[None]
        interp = (1.0 - a) * (1.0 - c) * q00 + a * (1.0 - c) * q10
        return interp + (1.0 - a) * c * q01 + a * c * q11

    def exchange(values):
        pieces = split_parts(values)
        spread = jnp.where(rank_hot[None, None], pieces[:, :, None, :], jnp.zeros((), BF16))
        packed = lax.dot_general(
            peer_mat, spread, (((0,), (3,)), ((), ())), preferred_element_type=F32
        )
        packed = packed[:, 0] + packed[:, 1]
        return lax.all_to_all(packed, "brick", 0, 0, tiled=True)

    local_state = state[:, 0]

    first_interp = interpolate(local_state)
    target_code = (target_cell + 1).astype(F32)
    received = exchange(jnp.concatenate([first_interp, target_code[None]], axis=0))
    slot_count = peer_count * capacity

    def flat_slots(values):
        return jnp.transpose(values, (1, 0, 2)).reshape(values.shape[1], slot_count)

    recv_cells = flat_slots(received[:, var_count:]).astype(jnp.int32)[0] - 1
    recv_i = jnp.floor_divide(recv_cells, col_count)
    recv_j = recv_cells - recv_i * col_count
    cell_mat = (
        recv_j[:, None] == jnp.arange(col_count, dtype=jnp.int32)[None, :]
    ).astype(jnp.float8_e4m3fn)
    cell_mat = lax.optimization_barrier(cell_mat)
    recv_row = jnp.arange(row_count, dtype=jnp.int32)[:, None] == recv_i[None]

    def spread_values(values):
        pieces = split_parts(flat_slots(values))
        return jnp.where(recv_row[None, None], pieces[:, :, None], jnp.zeros((), BF16))

    def to_cells(spread):
        return lax.dot_general(
            spread, cell_mat.astype(BF16), (((3,), (0,)), ((), ())), preferred_element_type=F32
        )

    first_spread = spread_values(received[:, :var_count])
    marks = jnp.broadcast_to(recv_row.astype(BF16)[None, None], (2, 1) + recv_row.shape)
    first_cells = to_cells(jnp.concatenate([first_spread, marks], axis=1))
    hit = first_cells[0, var_count] > 0.5

    def place(field, values, cells=None):
        if cells is None:
            cells = to_cells(spread_values(values))
        placed = join_parts(cells)
        return jnp.where(hit[None], placed, field)

    def fringe(field):
        return place(field, exchange(interpolate(field)))

    live_mask = (jnp.arange(col_count, dtype=jnp.int32) < brick_cols[0]).astype(F32)[None, None, :]

    def rhs(field):
        extended = with_halo(field, "span", 1, 1)
        upper = extended[:, 2:, :]
        lower = extended[:, :-2, :]
        right = shift_cols(field, True)
        left = shift_cols(field, False)
        diff_i = upper - lower
        diff_j = right - left
        laplace = upper + lower + right + left - 4.0 * field
        advect = sum(
            jacobian_i[:, w, None, None] * diff_i[w] + jacobian_j[:, w, None, None] * diff_j[w]
            for w in range(field.shape[0])
        )
        return (-0.5 * advect + viscosity * laplace) * live_mask

    section_zero = place(local_state, None, first_cells[:, :var_count])
    section_one = fringe(section_zero + time_step * rhs(section_zero))
    section_two = fringe(0.75 * section_zero + 0.25 * (section_one + time_step * rhs(section_one)))
    state_next = section_zero / 3.0 + 2.0 / 3.0 * (section_two + time_step * rhs(section_two))
    span_count = lax.axis_size("span")
    wall_dir = wall_angle.reshape(col_count)
    own_geom = jnp.stack(
        [(wall_patch.reshape(col_count) + 1).astype(F32), jnp.cos(wall_dir), jnp.sin(wall_dir)]
    )
    next_geom = lax.ppermute(own_geom, "span", [(i + 1, i) for i in range(span_count - 1)])
    xpos = (jnp.arange(col_count, dtype=F32) + 0.5) / col_count - 0.5
    live_row = live_mask[0, 0]

    def wall_partial(pressure, geom):
        patch = geom[0].astype(jnp.int32) - 1
        patch_hot = (patch[:, None] == jnp.arange(NP, dtype=jnp.int32)[None, :]).astype(F32)
        force_x = pressure * geom[1]
        force_y = pressure * geom[2]
        contrib = jnp.stack([force_x, force_y, xpos * force_y])
        return jnp.dot(contrib, patch_hot, precision=lax.Precision.HIGHEST)

    first = section_two[:, 0]
    diff_j = shift_cols(first, True) - shift_cols(first, False)
    laplace = section_two[4, 1] + shift_cols(first[4], True) + shift_cols(first[4], False)
    laplace = laplace - 4.0 * first[4]
    advect = jnp.dot(jacobian_i[4], section_two[:, 1], precision=lax.Precision.HIGHEST)
    advect = advect + jnp.dot(jacobian_j[4], diff_j, precision=lax.Precision.HIGHEST)
    own_rate = (-0.5 * advect + viscosity * laplace) * live_row
    own_pressure = section_zero[4, 0] / 3.0 + 2.0 / 3.0 * (first[4] + time_step * own_rate)
    last = section_two[:, -1]
    halo_rate = (0.5 * jnp.dot(jacobian_i[4], last, precision=lax.Precision.HIGHEST) + viscosity * last[4]) * live_row
    next_pressure = 2.0 / 3.0 * (time_step * halo_rate)
    partial_loads = wall_partial(own_pressure, own_geom) + wall_partial(next_pressure, next_geom)
    span_loads = lax.psum(partial_loads, "span")
    copies = jnp.broadcast_to(span_loads[None], (peer_count,) + span_loads.shape)
    gathered = lax.all_to_all(copies, "brick", 0, 0, tiled=True)
    loads = jnp.sum(gathered, axis=0) / col_count
    return (state_next[:, None], loads)


def solution(mesh):
    return jax.shard_map(
        shards,
        mesh=mesh,
        in_specs=(
            P(None, "brick", "span", None),
            P(),
            P(),
            P("brick"),
            P("brick", "span", None),
            P("brick", "span", None),
            P("brick", "span", None),
            P(None, "brick", "span", None),
            P("brick", "span", None),
            P("brick", "span", None),
        ),
        out_specs=(P(None, "brick", "span", None), P()),
        check_vma=False,
    )
```

```python
import jax
import jax.numpy as jnp
from jax import lax
from jax.sharding import PartitionSpec as P

NP = 16

viscosity = 0.1
time_step = 0.3

F32 = jnp.float32
BF16 = jnp.bfloat16


def with_halo(block, axis, dim, width):
    count = lax.axis_size(axis)
    forward = [(i, i + 1) for i in range(count - 1)]
    backward = [(target, source) for source, target in forward]
    low = lax.ppermute(
        lax.slice_in_dim(block, block.shape[dim] - width, None, axis=dim), axis, forward
    )
    high = lax.ppermute(lax.slice_in_dim(block, 0, width, axis=dim), axis, backward)
    return jnp.concatenate([low, block, high], axis=dim)


def shift_cols(field, forward):
    zero_col = jnp.zeros(field.shape[:-1] + (1,), field.dtype)
    if forward:
        return jnp.concatenate([field[..., 1:], zero_col], axis=-1)
    return jnp.concatenate([zero_col, field[..., :-1]], axis=-1)


def split_parts(x):
    hi = lax.reduce_precision(x, exponent_bits=8, mantissa_bits=7)
    lo = x - hi
    return jnp.stack([hi, lo]).astype(BF16)


def join_parts(parts):
    return parts[0] + parts[1]


def shards(
    state,
    jacobian_i,
    jacobian_j,
    brick_cols,
    fringe_peer,
    fringe_donor,
    fringe_target,
    fringe_frac,
    wall_patch,
    wall_angle,
):
    var_count = state.shape[0]
    row_count = state.shape[2]
    col_count = state.shape[3]
    peer_count = lax.axis_size("brick")
    fringe_rows = fringe_peer.shape[-1]
    capacity = 2 * fringe_rows // peer_count

    dest_peer = fringe_peer.reshape(fringe_rows)
    donor_cell = fringe_donor.reshape(fringe_rows)
    target_cell = fringe_target.reshape(fringe_rows)
    frac_a = fringe_frac[0].reshape(fringe_rows)
    frac_c = fringe_frac[1].reshape(fringe_rows)

    peer_hot = dest_peer[:, None] == jnp.arange(peer_count, dtype=jnp.int32)[None, :]
    peer_int = peer_hot.astype(jnp.int32)
    rank_in = jnp.sum(jnp.cumsum(peer_int, axis=0) * peer_int, axis=1) - 1
    peer_mat = peer_hot.astype(BF16)
    rank_hot = jnp.arange(capacity, dtype=jnp.int32)[:, None] == rank_in[None, :]

    donor_i = donor_cell // col_count
    donor_j = donor_cell % col_count
    col_mat = (jnp.arange(col_count, dtype=jnp.int32)[:, None] == donor_j[None, :]).astype(BF16)
    row_iota = jnp.arange(row_count, dtype=jnp.int32)[:, None]
    row_lo = row_iota == donor_i[None, :]
    row_hi = row_iota == donor_i[None, :] + 1

    def interpolate(field):
        shifted = jnp.concatenate([field[..., 1:], field[..., :1]], axis=-1)
        pieces = split_parts(jnp.stack([field, shifted]))
        picked = lax.dot_general(
            pieces, col_mat, (((4,), (0,)), ((), ())), preferred_element_type=F32
        )
        picked = join_parts(picked)
        at_lo = jnp.sum(jnp.where(row_lo[None, None], picked, 0.0), axis=2)
        at_hi = jnp.sum(jnp.where(row_hi[None, None], picked, 0.0), axis=2)
        q00, q01 = at_lo[0], at_lo[1]
        q10, q11 = at_hi[0], at_hi[1]
        a = frac_a[None]
        c = frac_c[None]
        interp = (1.0 - a) * (1.0 - c) * q00 + a * (1.0 - c) * q10
        return interp + (1.0 - a) * c * q01 + a * c * q11

    def exchange(values):
        pieces = split_parts(values)
        spread = jnp.where(rank_hot[None, None], pieces[:, :, None, :], jnp.zeros((), BF16))
        packed = lax.dot_general(
            peer_mat, spread, (((0,), (3,)), ((), ())), preferred_element_type=F32
        )
        packed = packed[:, 0] + packed[:, 1]
        return lax.all_to_all(packed, "brick", 0, 0, tiled=True)

    local_state = state[:, 0]

    first_interp = interpolate(local_state)
    target_code = (target_cell + 1).astype(F32)
    received = exchange(jnp.concatenate([first_interp, target_code[None]], axis=0))
    slot_count = peer_count * capacity

    def flat_slots(values):
        return jnp.transpose(values, (1, 0, 2)).reshape(values.shape[1], slot_count)

    recv_cells = flat_slots(received[:, var_count:]).astype(jnp.int32)[0] - 1
    recv_i = jnp.floor_divide(recv_cells, col_count)
    recv_j = recv_cells - recv_i * col_count
    cell_mat = (
        recv_j[:, None] == jnp.arange(col_count, dtype=jnp.int32)[None, :]
    ).astype(BF16)
    recv_row = jnp.arange(row_count, dtype=jnp.int32)[:, None] == recv_i[None]

    def spread_values(values):
        pieces = split_parts(flat_slots(values))
        return jnp.where(recv_row[None, None], pieces[:, :, None], jnp.zeros((), BF16))

    def to_cells(spread):
        return lax.dot_general(
            spread, cell_mat, (((3,), (0,)), ((), ())), preferred_element_type=F32
        )

    first_spread = spread_values(received[:, :var_count])
    marks = jnp.broadcast_to(recv_row.astype(BF16)[None, None], (2, 1) + recv_row.shape)
    first_cells = to_cells(jnp.concatenate([first_spread, marks], axis=1))
    hit = first_cells[0, var_count] > 0.5

    def place(field, values, cells=None):
        if cells is None:
            cells = to_cells(spread_values(values))
        placed = join_parts(cells)
        return jnp.where(hit[None], placed, field)

    def fringe(field):
        return place(field, exchange(interpolate(field)))

    live_mask = (jnp.arange(col_count, dtype=jnp.int32) < brick_cols[0]).astype(F32)[None, None, :]

    def rhs(field):
        extended = with_halo(field, "span", 1, 1)
        upper = extended[:, 2:, :]
        lower = extended[:, :-2, :]
        right = shift_cols(field, True)
        left = shift_cols(field, False)
        diff_i = upper - lower
        diff_j = right - left
        laplace = upper + lower + right + left - 4.0 * field
        advect = sum(
            jacobian_i[:, w, None, None] * diff_i[w] + jacobian_j[:, w, None, None] * diff_j[w]
            for w in range(field.shape[0])
        )
        return (-0.5 * advect + viscosity * laplace) * live_mask

    section_zero = place(local_state, None, first_cells[:, :var_count])
    section_one = fringe(section_zero + time_step * rhs(section_zero))
    section_two = fringe(0.75 * section_zero + 0.25 * (section_one + time_step * rhs(section_one)))
    state_next = section_zero / 3.0 + 2.0 / 3.0 * (section_two + time_step * rhs(section_two))
    span_count = lax.axis_size("span")
    wall_dir = wall_angle.reshape(col_count)
    own_geom = jnp.stack(
        [(wall_patch.reshape(col_count) + 1).astype(F32), jnp.cos(wall_dir), jnp.sin(wall_dir)]
    )
    next_geom = lax.ppermute(own_geom, "span", [(i + 1, i) for i in range(span_count - 1)])
    xpos = (jnp.arange(col_count, dtype=F32) + 0.5) / col_count - 0.5
    live_row = live_mask[0, 0]

    def wall_partial(pressure, geom):
        patch = geom[0].astype(jnp.int32) - 1
        patch_hot = (patch[:, None] == jnp.arange(NP, dtype=jnp.int32)[None, :]).astype(F32)
        force_x = pressure * geom[1]
        force_y = pressure * geom[2]
        contrib = jnp.stack([force_x, force_y, xpos * force_y])
        return jnp.dot(contrib, patch_hot, precision=lax.Precision.HIGHEST)

    first = section_two[:, 0]
    diff_j = shift_cols(first, True) - shift_cols(first, False)
    laplace = section_two[4, 1] + shift_cols(first[4], True) + shift_cols(first[4], False)
    laplace = laplace - 4.0 * first[4]
    advect = jnp.dot(jacobian_i[4], section_two[:, 1], precision=lax.Precision.HIGHEST)
    advect = advect + jnp.dot(jacobian_j[4], diff_j, precision=lax.Precision.HIGHEST)
    own_rate = (-0.5 * advect + viscosity * laplace) * live_row
    own_pressure = section_zero[4, 0] / 3.0 + 2.0 / 3.0 * (first[4] + time_step * own_rate)
    last = section_two[:, -1]
    halo_rate = (0.5 * jnp.dot(jacobian_i[4], last, precision=lax.Precision.HIGHEST) + viscosity * last[4]) * live_row
    next_pressure = 2.0 / 3.0 * (time_step * halo_rate)
    partial_loads = wall_partial(own_pressure, own_geom) + wall_partial(next_pressure, next_geom)
    span_loads = lax.psum(partial_loads, "span")
    copies = jnp.broadcast_to(span_loads[None], (peer_count,) + span_loads.shape)
    gathered = lax.all_to_all(copies, "brick", 0, 0, tiled=True)
    loads = jnp.sum(gathered, axis=0) / col_count
    return (state_next[:, None], loads)


def solution(mesh):
    return jax.shard_map(
        shards,
        mesh=mesh,
        in_specs=(
            P(None, "brick", "span", None),
            P(),
            P(),
            P("brick"),
            P("brick", "span", None),
            P("brick", "span", None),
            P("brick", "span", None),
            P(None, "brick", "span", None),
            P("brick", "span", None),
            P("brick", "span", None),
        ),
        out_specs=(P(None, "brick", "span", None), P()),
        check_vma=False,
    )
```

```python
import jax
import jax.numpy as jnp
from jax import lax
from jax.sharding import PartitionSpec as P

NP = 16

viscosity = 0.1
time_step = 0.3

F32 = jnp.float32
BF16 = jnp.bfloat16


def with_halo(block, axis, dim, width):
    count = lax.axis_size(axis)
    forward = [(i, i + 1) for i in range(count - 1)]
    backward = [(target, source) for source, target in forward]
    low = lax.ppermute(
        lax.slice_in_dim(block, block.shape[dim] - width, None, axis=dim), axis, forward
    )
    high = lax.ppermute(lax.slice_in_dim(block, 0, width, axis=dim), axis, backward)
    return jnp.concatenate([low, block, high], axis=dim)


def shift_cols(field, forward):
    zero_col = jnp.zeros(field.shape[:-1] + (1,), field.dtype)
    if forward:
        return jnp.concatenate([field[..., 1:], zero_col], axis=-1)
    return jnp.concatenate([zero_col, field[..., :-1]], axis=-1)


def split_parts(x):
    hi = lax.reduce_precision(x, exponent_bits=8, mantissa_bits=7)
    lo = x - hi
    return jnp.stack([hi, lo]).astype(BF16)


def join_parts(parts):
    return parts[0] + parts[1]


def shards(
    state,
    jacobian_i,
    jacobian_j,
    brick_cols,
    fringe_peer,
    fringe_donor,
    fringe_target,
    fringe_frac,
    wall_patch,
    wall_angle,
):
    var_count = state.shape[0]
    row_count = state.shape[2]
    col_count = state.shape[3]
    peer_count = lax.axis_size("brick")
    fringe_rows = fringe_peer.shape[-1]
    capacity = 2 * fringe_rows // peer_count

    dest_peer = fringe_peer.reshape(fringe_rows)
    donor_cell = fringe_donor.reshape(fringe_rows)
    target_cell = fringe_target.reshape(fringe_rows)
    frac_a = fringe_frac[0].reshape(fringe_rows)
    frac_c = fringe_frac[1].reshape(fringe_rows)

    peer_hot = dest_peer[:, None] == jnp.arange(peer_count, dtype=jnp.int32)[None, :]
    peer_int = peer_hot.astype(jnp.int32)
    rank_in = jnp.sum(jnp.cumsum(peer_int, axis=0) * peer_int, axis=1) - 1
    peer_mat = peer_hot.astype(BF16)
    rank_hot = jnp.arange(capacity, dtype=jnp.int32)[:, None] == rank_in[None, :]

    donor_i = donor_cell // col_count
    donor_j = donor_cell % col_count
    col_mat = (jnp.arange(col_count, dtype=jnp.int32)[:, None] == donor_j[None, :]).astype(BF16)
    row_iota = jnp.arange(row_count, dtype=jnp.int32)[:, None]
    row_lo = row_iota == donor_i[None, :]
    row_hi = row_iota == donor_i[None, :] + 1

    def interpolate(field):
        shifted = jnp.concatenate([field[..., 1:], field[..., :1]], axis=-1)
        pieces = split_parts(jnp.stack([field, shifted]))
        picked = lax.dot_general(
            pieces, col_mat, (((4,), (0,)), ((), ())), preferred_element_type=F32
        )
        picked = join_parts(picked)
        at_lo = jnp.sum(jnp.where(row_lo[None, None], picked, 0.0), axis=2)
        at_hi = jnp.sum(jnp.where(row_hi[None, None], picked, 0.0), axis=2)
        q00, q01 = at_lo[0], at_lo[1]
        q10, q11 = at_hi[0], at_hi[1]
        a = frac_a[None]
        c = frac_c[None]
        interp = (1.0 - a) * (1.0 - c) * q00 + a * (1.0 - c) * q10
        return interp + (1.0 - a) * c * q01 + a * c * q11

    def exchange(values):
        pieces = split_parts(values)
        spread = jnp.where(rank_hot[None, None], pieces[:, :, None, :], jnp.zeros((), BF16))
        packed = lax.dot_general(
            peer_mat, spread, (((0,), (3,)), ((), ())), preferred_element_type=F32
        )
        packed = packed[:, 0] + packed[:, 1]
        flat = packed.reshape(peer_count, 1, packed.shape[1] * packed.shape[2])
        moved = lax.all_to_all(flat, "brick", 0, 0, tiled=True)
        return moved.reshape(packed.shape)

    local_state = state[:, 0]

    first_interp = interpolate(local_state)
    target_code = (target_cell + 1).astype(F32)
    received = exchange(jnp.concatenate([first_interp, target_code[None]], axis=0))
    slot_count = peer_count * capacity

    def flat_slots(values):
        return jnp.transpose(values, (1, 0, 2)).reshape(values.shape[1], slot_count)

    recv_cells = flat_slots(received[:, var_count:]).astype(jnp.int32)[0] - 1
    recv_i = jnp.floor_divide(recv_cells, col_count)
    recv_j = recv_cells - recv_i * col_count
    cell_mat = (
        recv_j[:, None] == jnp.arange(col_count, dtype=jnp.int32)[None, :]
    ).astype(BF16)
    recv_row = jnp.arange(row_count, dtype=jnp.int32)[:, None] == recv_i[None]

    def spread_values(values):
        pieces = split_parts(flat_slots(values))
        return jnp.where(recv_row[None, None], pieces[:, :, None], jnp.zeros((), BF16))

    def to_cells(spread):
        return lax.dot_general(
            spread, cell_mat, (((3,), (0,)), ((), ())), preferred_element_type=F32
        )

    first_spread = spread_values(received[:, :var_count])
    marks = jnp.broadcast_to(recv_row.astype(BF16)[None, None], (2, 1) + recv_row.shape)
    first_cells = to_cells(jnp.concatenate([first_spread, marks], axis=1))
    hit = first_cells[0, var_count] > 0.5

    def place(field, values, cells=None):
        if cells is None:
            cells = to_cells(spread_values(values))
        placed = join_parts(cells)
        return jnp.where(hit[None], placed, field)

    def fringe(field):
        return place(field, exchange(interpolate(field)))

    live_mask = (jnp.arange(col_count, dtype=jnp.int32) < brick_cols[0]).astype(F32)[None, None, :]

    def rhs(field):
        extended = with_halo(field, "span", 1, 1)
        upper = extended[:, 2:, :]
        lower = extended[:, :-2, :]
        right = shift_cols(field, True)
        left = shift_cols(field, False)
        diff_i = upper - lower
        diff_j = right - left
        laplace = upper + lower + right + left - 4.0 * field
        advect = sum(
            jacobian_i[:, w, None, None] * diff_i[w] + jacobian_j[:, w, None, None] * diff_j[w]
            for w in range(field.shape[0])
        )
        return (-0.5 * advect + viscosity * laplace) * live_mask

    section_zero = place(local_state, None, first_cells[:, :var_count])
    section_one = fringe(section_zero + time_step * rhs(section_zero))
    section_two = fringe(0.75 * section_zero + 0.25 * (section_one + time_step * rhs(section_one)))
    state_next = section_zero / 3.0 + 2.0 / 3.0 * (section_two + time_step * rhs(section_two))
    span_count = lax.axis_size("span")
    wall_dir = wall_angle.reshape(col_count)
    own_geom = jnp.stack(
        [(wall_patch.reshape(col_count) + 1).astype(F32), jnp.cos(wall_dir), jnp.sin(wall_dir)]
    )
    next_geom = lax.ppermute(own_geom, "span", [(i + 1, i) for i in range(span_count - 1)])
    xpos = (jnp.arange(col_count, dtype=F32) + 0.5) / col_count - 0.5
    live_row = live_mask[0, 0]

    def wall_partial(pressure, geom):
        patch = geom[0].astype(jnp.int32) - 1
        patch_hot = (patch[:, None] == jnp.arange(NP, dtype=jnp.int32)[None, :]).astype(F32)
        force_x = pressure * geom[1]
        force_y = pressure * geom[2]
        contrib = jnp.stack([force_x, force_y, xpos * force_y])
        return jnp.dot(contrib, patch_hot, precision=lax.Precision.HIGHEST)

    first = section_two[:, 0]
    diff_j = shift_cols(first, True) - shift_cols(first, False)
    laplace = section_two[4, 1] + shift_cols(first[4], True) + shift_cols(first[4], False)
    laplace = laplace - 4.0 * first[4]
    advect = jnp.dot(jacobian_i[4], section_two[:, 1], precision=lax.Precision.HIGHEST)
    advect = advect + jnp.dot(jacobian_j[4], diff_j, precision=lax.Precision.HIGHEST)
    own_rate = (-0.5 * advect + viscosity * laplace) * live_row
    own_pressure = section_zero[4, 0] / 3.0 + 2.0 / 3.0 * (first[4] + time_step * own_rate)
    last = section_two[:, -1]
    halo_rate = (0.5 * jnp.dot(jacobian_i[4], last, precision=lax.Precision.HIGHEST) + viscosity * last[4]) * live_row
    next_pressure = 2.0 / 3.0 * (time_step * halo_rate)
    partial_loads = wall_partial(own_pressure, own_geom) + wall_partial(next_pressure, next_geom)
    span_loads = lax.psum(partial_loads, "span")
    copies = jnp.broadcast_to(span_loads[None], (peer_count,) + span_loads.shape)
    gathered = lax.all_to_all(copies, "brick", 0, 0, tiled=True)
    loads = jnp.sum(gathered, axis=0) / col_count
    return (state_next[:, None], loads)


def solution(mesh):
    return jax.shard_map(
        shards,
        mesh=mesh,
        in_specs=(
            P(None, "brick", "span", None),
            P(),
            P(),
            P("brick"),
            P("brick", "span", None),
            P("brick", "span", None),
            P("brick", "span", None),
            P(None, "brick", "span", None),
            P("brick", "span", None),
            P("brick", "span", None),
        ),
        out_specs=(P(None, "brick", "span", None), P()),
        check_vma=False,
    )
```

```python
import jax
import jax.numpy as jnp
from jax import lax
from jax.sharding import PartitionSpec as P

NP = 16

viscosity = 0.1
time_step = 0.3

F32 = jnp.float32
BF16 = jnp.bfloat16


def with_halo(block, axis, dim, width):
    count = lax.axis_size(axis)
    forward = [(i, i + 1) for i in range(count - 1)]
    backward = [(target, source) for source, target in forward]
    low = lax.ppermute(
        lax.slice_in_dim(block, block.shape[dim] - width, None, axis=dim), axis, forward
    )
    high = lax.ppermute(lax.slice_in_dim(block, 0, width, axis=dim), axis, backward)
    return jnp.concatenate([low, block, high], axis=dim)


def shift_cols(field, forward):
    zero_col = jnp.zeros(field.shape[:-1] + (1,), field.dtype)
    if forward:
        return jnp.concatenate([field[..., 1:], zero_col], axis=-1)
    return jnp.concatenate([zero_col, field[..., :-1]], axis=-1)


def split_parts(x):
    hi = lax.reduce_precision(x, exponent_bits=8, mantissa_bits=7)
    lo = x - hi
    return jnp.stack([hi, lo]).astype(BF16)


def join_parts(parts):
    return parts[0] + parts[1]


def shards(
    state,
    jacobian_i,
    jacobian_j,
    brick_cols,
    fringe_peer,
    fringe_donor,
    fringe_target,
    fringe_frac,
    wall_patch,
    wall_angle,
):
    var_count = state.shape[0]
    row_count = state.shape[2]
    col_count = state.shape[3]
    peer_count = lax.axis_size("brick")
    fringe_rows = fringe_peer.shape[-1]
    capacity = 2 * fringe_rows // peer_count

    dest_peer = fringe_peer.reshape(fringe_rows)
    donor_cell = fringe_donor.reshape(fringe_rows)
    target_cell = fringe_target.reshape(fringe_rows)
    frac_a = fringe_frac[0].reshape(fringe_rows)
    frac_c = fringe_frac[1].reshape(fringe_rows)

    peer_hot = dest_peer[:, None] == jnp.arange(peer_count, dtype=jnp.int32)[None, :]
    peer_int = peer_hot.astype(jnp.int32)
    rank_in = jnp.sum(jnp.cumsum(peer_int, axis=0) * peer_int, axis=1) - 1
    peer_mat = peer_hot.astype(BF16)
    rank_hot = jnp.arange(capacity, dtype=jnp.int32)[:, None] == rank_in[None, :]

    donor_i = donor_cell // col_count
    donor_j = donor_cell % col_count
    col_mat = (jnp.arange(col_count, dtype=jnp.int32)[:, None] == donor_j[None, :]).astype(BF16)
    row_iota = jnp.arange(row_count, dtype=jnp.int32)[:, None]
    row_lo = row_iota == donor_i[None, :]
    row_hi = row_iota == donor_i[None, :] + 1

    def interpolate(field):
        shifted = jnp.concatenate([field[..., 1:], field[..., :1]], axis=-1)
        pieces = split_parts(jnp.stack([field, shifted]))
        picked = lax.dot_general(
            pieces, col_mat, (((4,), (0,)), ((), ())), preferred_element_type=F32
        )
        picked = join_parts(picked)
        at_lo = jnp.sum(jnp.where(row_lo[None, None], picked, 0.0), axis=2)
        at_hi = jnp.sum(jnp.where(row_hi[None, None], picked, 0.0), axis=2)
        q00, q01 = at_lo[0], at_lo[1]
        q10, q11 = at_hi[0], at_hi[1]
        a = frac_a[None]
        c = frac_c[None]
        interp = (1.0 - a) * (1.0 - c) * q00 + a * (1.0 - c) * q10
        return interp + (1.0 - a) * c * q01 + a * c * q11

    def exchange(values):
        pieces = split_parts(values)
        spread = jnp.where(rank_hot[None, None], pieces[:, :, None, :], jnp.zeros((), BF16))
        packed = lax.dot_general(
            peer_mat, spread, (((0,), (3,)), ((), ())), preferred_element_type=F32
        )
        packed = packed[:, 0] + packed[:, 1]
        flat = packed.reshape(peer_count, 1, packed.shape[1] * packed.shape[2])
        moved = lax.all_to_all(flat, "brick", 0, 0, tiled=True)
        return moved.reshape(packed.shape)

    local_state = state[:, 0]

    first_interp = interpolate(local_state)
    target_code = (target_cell + 1).astype(F32)
    received = exchange(jnp.concatenate([first_interp, target_code[None]], axis=0))
    slot_count = peer_count * capacity

    def flat_slots(values):
        return jnp.transpose(values, (1, 0, 2)).reshape(values.shape[1], slot_count)

    recv_cells = flat_slots(received[:, var_count:]).astype(jnp.int32)[0] - 1
    recv_i = jnp.floor_divide(recv_cells, col_count)
    recv_j = recv_cells - recv_i * col_count
    cell_mat = (
        recv_j[:, None] == jnp.arange(col_count, dtype=jnp.int32)[None, :]
    ).astype(BF16)
    recv_row = jnp.arange(row_count, dtype=jnp.int32)[:, None] == recv_i[None]

    def spread_values(values):
        pieces = split_parts(flat_slots(values))
        return jnp.where(recv_row[None, None], pieces[:, :, None], jnp.zeros((), BF16))

    def to_cells(spread):
        return lax.dot_general(
            spread, cell_mat, (((3,), (0,)), ((), ())), preferred_element_type=F32
        )

    first_spread = spread_values(received[:, :var_count])
    marks = jnp.broadcast_to(recv_row.astype(BF16)[None, None], (2, 1) + recv_row.shape)
    first_cells = to_cells(jnp.concatenate([first_spread, marks], axis=1))
    hit = first_cells[0, var_count] > 0.5

    def place(field, values, cells=None):
        if cells is None:
            cells = to_cells(spread_values(values))
        placed = join_parts(cells)
        return jnp.where(hit[None], placed, field)

    def fringe(field):
        return place(field, exchange(interpolate(field)))

    live_mask = (jnp.arange(col_count, dtype=jnp.int32) < brick_cols[0]).astype(F32)[None, None, :]

    def rhs(field):
        extended = with_halo(field, "span", 1, 1)
        upper = extended[:, 2:, :]
        lower = extended[:, :-2, :]
        right = shift_cols(field, True)
        left = shift_cols(field, False)
        diff_i = upper - lower
        diff_j = right - left
        laplace = upper + lower + right + left - 4.0 * field
        advect = sum(
            jacobian_i[:, w, None, None] * diff_i[w] + jacobian_j[:, w, None, None] * diff_j[w]
            for w in range(field.shape[0])
        )
        return (-0.5 * advect + viscosity * laplace) * live_mask

    section_zero = place(local_state, None, first_cells[:, :var_count])
    section_one = fringe(section_zero + time_step * rhs(section_zero))
    section_two = fringe(0.75 * section_zero + 0.25 * (section_one + time_step * rhs(section_one)))
    state_next = section_zero / 3.0 + 2.0 / 3.0 * (section_two + time_step * rhs(section_two))
    span_count = lax.axis_size("span")
    wall_dir = wall_angle.reshape(col_count)
    own_geom = jnp.stack(
        [(wall_patch.reshape(col_count) + 1).astype(F32), jnp.cos(wall_dir), jnp.sin(wall_dir)]
    )
    next_geom = lax.ppermute(own_geom, "span", [(i + 1, i) for i in range(span_count - 1)])
    xpos = (jnp.arange(col_count, dtype=F32) + 0.5) / col_count - 0.5
    live_row = live_mask[0, 0]

    def wall_partial(pressure, geom):
        patch = geom[0].astype(jnp.int32) - 1
        patch_hot = (patch[:, None] == jnp.arange(NP, dtype=jnp.int32)[None, :]).astype(F32)
        force_x = pressure * geom[1]
        force_y = pressure * geom[2]
        contrib = jnp.stack([force_x, force_y, xpos * force_y])
        return jnp.dot(contrib, patch_hot, precision=lax.Precision.HIGHEST)

    first = section_two[:, 0]
    diff_j = shift_cols(first, True) - shift_cols(first, False)
    laplace = section_two[4, 1] + shift_cols(first[4], True) + shift_cols(first[4], False)
    laplace = laplace - 4.0 * first[4]
    advect = jnp.dot(jacobian_i[4], section_two[:, 1], precision=lax.Precision.HIGHEST)
    advect = advect + jnp.dot(jacobian_j[4], diff_j, precision=lax.Precision.HIGHEST)
    own_rate = (-0.5 * advect + viscosity * laplace) * live_row
    own_pressure = section_zero[4, 0] / 3.0 + 2.0 / 3.0 * (first[4] + time_step * own_rate)
    last = section_two[:, -1]
    halo_rate = (0.5 * jnp.dot(jacobian_i[4], last, precision=lax.Precision.HIGHEST) + viscosity * last[4]) * live_row
    next_pressure = 2.0 / 3.0 * (time_step * halo_rate)
    partial_loads = wall_partial(own_pressure, own_geom) + wall_partial(next_pressure, next_geom)
    span_loads = lax.psum(partial_loads, "span")
    copies = jnp.broadcast_to(span_loads.reshape(1, 1, -1), (peer_count, 1, span_loads.size))
    gathered = lax.all_to_all(copies, "brick", 0, 0, tiled=True)
    loads = jnp.sum(gathered, axis=(0, 1)).reshape(span_loads.shape) / col_count
    return (state_next[:, None], loads)


def solution(mesh):
    return jax.shard_map(
        shards,
        mesh=mesh,
        in_specs=(
            P(None, "brick", "span", None),
            P(),
            P(),
            P("brick"),
            P("brick", "span", None),
            P("brick", "span", None),
            P("brick", "span", None),
            P(None, "brick", "span", None),
            P("brick", "span", None),
            P("brick", "span", None),
        ),
        out_specs=(P(None, "brick", "span", None), P()),
        check_vma=False,
    )
```

```python
import jax
import jax.numpy as jnp
from jax import lax
from jax.sharding import PartitionSpec as P

NP = 16

viscosity = 0.1
time_step = 0.3

F32 = jnp.float32
BF16 = jnp.bfloat16


def with_halo(block, axis, dim, width):
    count = lax.axis_size(axis)
    forward = [(i, i + 1) for i in range(count - 1)]
    backward = [(target, source) for source, target in forward]
    low = lax.ppermute(
        lax.slice_in_dim(block, block.shape[dim] - width, None, axis=dim), axis, forward
    )
    high = lax.ppermute(lax.slice_in_dim(block, 0, width, axis=dim), axis, backward)
    return jnp.concatenate([low, block, high], axis=dim)


def shift_cols(field, forward):
    zero_col = jnp.zeros(field.shape[:-1] + (1,), field.dtype)
    if forward:
        return jnp.concatenate([field[..., 1:], zero_col], axis=-1)
    return jnp.concatenate([zero_col, field[..., :-1]], axis=-1)


def split_parts(x):
    hi = lax.reduce_precision(x, exponent_bits=8, mantissa_bits=7)
    lo = x - hi
    return jnp.stack([hi, lo]).astype(BF16)


def join_parts(parts):
    return parts[0] + parts[1]


def shards(
    state,
    jacobian_i,
    jacobian_j,
    brick_cols,
    fringe_peer,
    fringe_donor,
    fringe_target,
    fringe_frac,
    wall_patch,
    wall_angle,
):
    var_count = state.shape[0]
    row_count = state.shape[2]
    col_count = state.shape[3]
    peer_count = lax.axis_size("brick")
    fringe_rows = fringe_peer.shape[-1]
    capacity = 2 * fringe_rows // peer_count

    dest_peer = fringe_peer.reshape(fringe_rows)
    donor_cell = fringe_donor.reshape(fringe_rows)
    target_cell = fringe_target.reshape(fringe_rows)
    frac_a = fringe_frac[0].reshape(fringe_rows)
    frac_c = fringe_frac[1].reshape(fringe_rows)

    peer_hot = dest_peer[:, None] == jnp.arange(peer_count, dtype=jnp.int32)[None, :]
    peer_int = peer_hot.astype(jnp.int32)
    rank_in = jnp.sum(jnp.cumsum(peer_int, axis=0) * peer_int, axis=1) - 1
    peer_mat = peer_hot.astype(BF16)
    rank_hot = jnp.arange(capacity, dtype=jnp.int32)[:, None] == rank_in[None, :]

    donor_i = donor_cell // col_count
    donor_j = donor_cell % col_count
    col_mat = (jnp.arange(col_count, dtype=jnp.int32)[:, None] == donor_j[None, :]).astype(BF16)
    row_iota = jnp.arange(row_count, dtype=jnp.int32)[:, None]
    row_lo = row_iota == donor_i[None, :]
    row_hi = row_iota == donor_i[None, :] + 1

    next_col_mat = (
        jnp.arange(col_count, dtype=jnp.int32)[:, None] == donor_j[None, :] + 1
    ).astype(BF16)

    def interpolate(field, select_next=False):
        if select_next:
            pieces = split_parts(field)
            picked = jnp.stack(
                [
                    lax.dot_general(
                        pieces, mat, (((3,), (0,)), ((), ())), preferred_element_type=F32
                    )
                    for mat in (col_mat, next_col_mat)
                ],
                axis=1,
            )
        else:
            shifted = jnp.concatenate([field[..., 1:], field[..., :1]], axis=-1)
            pieces = split_parts(jnp.stack([field, shifted]))
            picked = lax.dot_general(
                pieces, col_mat, (((4,), (0,)), ((), ())), preferred_element_type=F32
            )
        picked = join_parts(picked)
        at_lo = jnp.sum(jnp.where(row_lo[None, None], picked, 0.0), axis=2)
        at_hi = jnp.sum(jnp.where(row_hi[None, None], picked, 0.0), axis=2)
        q00, q01 = at_lo[0], at_lo[1]
        q10, q11 = at_hi[0], at_hi[1]
        a = frac_a[None]
        c = frac_c[None]
        interp = (1.0 - a) * (1.0 - c) * q00 + a * (1.0 - c) * q10
        return interp + (1.0 - a) * c * q01 + a * c * q11

    def exchange(values):
        pieces = split_parts(values)
        spread = jnp.where(rank_hot[None, None], pieces[:, :, None, :], jnp.zeros((), BF16))
        packed = lax.dot_general(
            peer_mat, spread, (((0,), (3,)), ((), ())), preferred_element_type=F32
        )
        packed = packed[:, 0] + packed[:, 1]
        flat = packed.reshape(peer_count, 1, packed.shape[1] * packed.shape[2])
        moved = lax.all_to_all(flat, "brick", 0, 0, tiled=True)
        return moved.reshape(packed.shape)

    local_state = state[:, 0]

    first_interp = interpolate(local_state, select_next=True)
    target_code = (target_cell + 1).astype(F32)
    received = exchange(jnp.concatenate([first_interp, target_code[None]], axis=0))
    slot_count = peer_count * capacity

    def flat_slots(values):
        return jnp.transpose(values, (1, 0, 2)).reshape(values.shape[1], slot_count)

    recv_cells = flat_slots(received[:, var_count:]).astype(jnp.int32)[0] - 1
    recv_i = jnp.floor_divide(recv_cells, col_count)
    recv_j = recv_cells - recv_i * col_count
    cell_mat = (
        recv_j[:, None] == jnp.arange(col_count, dtype=jnp.int32)[None, :]
    ).astype(BF16)
    recv_row = jnp.arange(row_count, dtype=jnp.int32)[:, None] == recv_i[None]

    def spread_values(values):
        pieces = split_parts(flat_slots(values))
        return jnp.where(recv_row[None, None], pieces[:, :, None], jnp.zeros((), BF16))

    def to_cells(spread):
        return lax.dot_general(
            spread, cell_mat, (((3,), (0,)), ((), ())), preferred_element_type=F32
        )

    first_spread = spread_values(received[:, :var_count])
    marks = jnp.broadcast_to(recv_row.astype(BF16)[None, None], (2, 1) + recv_row.shape)
    first_cells = to_cells(jnp.concatenate([first_spread, marks], axis=1))
    hit = first_cells[0, var_count] > 0.5

    def place(field, values, cells=None):
        if cells is None:
            cells = to_cells(spread_values(values))
        placed = join_parts(cells)
        return jnp.where(hit[None], placed, field)

    def fringe(field):
        return place(field, exchange(interpolate(field)))

    live_mask = (jnp.arange(col_count, dtype=jnp.int32) < brick_cols[0]).astype(F32)[None, None, :]

    def rhs(field):
        extended = with_halo(field, "span", 1, 1)
        upper = extended[:, 2:, :]
        lower = extended[:, :-2, :]
        right = shift_cols(field, True)
        left = shift_cols(field, False)
        diff_i = upper - lower
        diff_j = right - left
        laplace = upper + lower + right + left - 4.0 * field
        advect = sum(
            jacobian_i[:, w, None, None] * diff_i[w] + jacobian_j[:, w, None, None] * diff_j[w]
            for w in range(field.shape[0])
        )
        return (-0.5 * advect + viscosity * laplace) * live_mask

    section_zero = place(local_state, None, first_cells[:, :var_count])
    section_one = fringe(section_zero + time_step * rhs(section_zero))
    section_two = fringe(0.75 * section_zero + 0.25 * (section_one + time_step * rhs(section_one)))
    state_next = section_zero / 3.0 + 2.0 / 3.0 * (section_two + time_step * rhs(section_two))
    span_count = lax.axis_size("span")
    wall_dir = wall_angle.reshape(col_count)
    own_geom = jnp.stack(
        [(wall_patch.reshape(col_count) + 1).astype(F32), jnp.cos(wall_dir), jnp.sin(wall_dir)]
    )
    next_geom = lax.ppermute(own_geom, "span", [(i + 1, i) for i in range(span_count - 1)])
    xpos = (jnp.arange(col_count, dtype=F32) + 0.5) / col_count - 0.5
    live_row = live_mask[0, 0]

    def wall_partial(pressure, geom):
        patch = geom[0].astype(jnp.int32) - 1
        patch_hot = (patch[:, None] == jnp.arange(NP, dtype=jnp.int32)[None, :]).astype(F32)
        force_x = pressure * geom[1]
        force_y = pressure * geom[2]
        contrib = jnp.stack([force_x, force_y, xpos * force_y])
        return jnp.dot(contrib, patch_hot, precision=lax.Precision.HIGHEST)

    first = section_two[:, 0]
    diff_j = shift_cols(first, True) - shift_cols(first, False)
    laplace = section_two[4, 1] + shift_cols(first[4], True) + shift_cols(first[4], False)
    laplace = laplace - 4.0 * first[4]
    advect = jnp.dot(jacobian_i[4], section_two[:, 1], precision=lax.Precision.HIGHEST)
    advect = advect + jnp.dot(jacobian_j[4], diff_j, precision=lax.Precision.HIGHEST)
    own_rate = (-0.5 * advect + viscosity * laplace) * live_row
    own_pressure = section_zero[4, 0] / 3.0 + 2.0 / 3.0 * (first[4] + time_step * own_rate)
    last = section_two[:, -1]
    halo_rate = (0.5 * jnp.dot(jacobian_i[4], last, precision=lax.Precision.HIGHEST) + viscosity * last[4]) * live_row
    next_pressure = 2.0 / 3.0 * (time_step * halo_rate)
    partial_loads = wall_partial(own_pressure, own_geom) + wall_partial(next_pressure, next_geom)
    span_loads = lax.psum(partial_loads, "span")
    copies = jnp.broadcast_to(span_loads.reshape(1, 1, -1), (peer_count, 1, span_loads.size))
    gathered = lax.all_to_all(copies, "brick", 0, 0, tiled=True)
    loads = jnp.sum(gathered, axis=(0, 1)).reshape(span_loads.shape) / col_count
    return (state_next[:, None], loads)


def solution(mesh):
    return jax.shard_map(
        shards,
        mesh=mesh,
        in_specs=(
            P(None, "brick", "span", None),
            P(),
            P(),
            P("brick"),
            P("brick", "span", None),
            P("brick", "span", None),
            P("brick", "span", None),
            P(None, "brick", "span", None),
            P("brick", "span", None),
            P("brick", "span", None),
        ),
        out_specs=(P(None, "brick", "span", None), P()),
        check_vma=False,
    )
```
